256 devices in a mesh: cfg: 2 (over z_lo), seq: 16 (over z_hi, x), wblk: 8 (over y, core).
Axes of the slice: x: 4, y: 4, z: 8 (z_hi: 4, z_lo: 2; z = z_hi * 2 + z_lo), core: 2. Of those that a mesh axis runs over, the one named last changes fastest.
Arguments:
- text_tokens: bfloat16 [2, 2, 512, 3072], P('cfg', None, 'seq', 'wblk'), may hold values from -16 to 16
- image_tokens: bfloat16 [2, 4096, 3072], P(None, 'seq', 'wblk'), may hold values from -16 to 16
- pooled_vector: float32 [2, 3072], P('cfg', 'seq'), may hold values from -6 to 6
- mod_weight: bfloat16 [3072, 3, 3072], P('seq', None, 'wblk'), may hold values from -0.109375 to 0.109375
- qkv_weight: bfloat16 [3072, 3, 16, 128], P('seq', None, 'wblk'), may hold values from -0.109375 to 0.109375
- up_weight: bfloat16 [3072, 6144], P('seq', 'wblk'), may hold values from -0.109375 to 0.109375
- query_gain: float32 [128], replicated, may hold values from 0.6 to 10
- key_gain: float32 [128], replicated, may hold values from 0.6 to 10
- attn_weight: bfloat16 [2048, 3072], P('wblk', 'seq'), may hold values from -0.125 to 0.125
- down_weight: bfloat16 [6144, 3072], P('wblk', 'seq'), may hold values from -0.078125 to 0.078125
- lengths: int32 [2], replicated, may hold values from 1 to 512, as said below
- timestep: int32 [1], replicated, may hold values from 0 to 27
Outputs:
- text_out: bfloat16 [2, 2, 512, 3072], P('cfg', None, 'seq', 'wblk')
- velocity: float32 [2, 4096, 3072], P('cfg', 'seq', 'wblk')
- new_image: float32 [2, 4096, 3072], P('cfg', 'seq', 'wblk')
The draws below stay inside these ranges and needn't reach their ends.
Inputs may be any that keep to these rules, and one draw needn't show every extreme that they name: `lengths`: some prompt has all 512 text tokens live in every draw.
All inputs are finite; a program needn't handle non-finite values.
Results may differ from the reference program's by a relative error of at most 0.025.
Values may be sent and summed in bfloat16 or wider, within the bound.
No kernel may reach another device: no remote copies, remote signals or barrier semaphores. Data moves between devices by JAX's collectives and lax.ppermute only.
A program may use at most 128 MiB of HBM per device.

```python
import math
import jax
import jax.numpy as jnp
from jax import lax

D = 3072
HEADS = 16
HD = 128
MLP = 6144
TXT = 512
GRID = 64
PROMPTS = 2
STEPS = 28
IMG = 4096
N_WBLK = 8


def gain_drawn(key):
    return jax.random.uniform(jax.random.fold_in(key, 14), (HD,), jnp.float32, 0.6, 1.8)


def draw_query_gain(key, part):
    return gain_drawn(jax.random.fold_in(key, 1))


def draw_key_gain(key, part):
    return gain_drawn(jax.random.fold_in(key, 2))


def draw_lengths(key, part):
    drawn_lengths = jax.random.randint(jax.random.fold_in(key, 3), (PROMPTS,), 1, TXT + 1)
    longest = jax.random.randint(jax.random.fold_in(key, 4), (), 0, PROMPTS)
    return jnp.where(jnp.arange(PROMPTS, dtype=jnp.int32) == longest, TXT, drawn_lengths).astype(jnp.int32)


def feature_tokens(key, shape):
    position = jnp.arange(D, dtype=jnp.float32) / (D - 1)
    ramp = jnp.exp(jnp.log(0.5) + (jnp.log(3.0) - jnp.log(0.5)) * position)
    values = jnp.clip(jax.random.normal(key, shape, jnp.float32), -4.0, 4.0)
    return (values * ramp).astype(jnp.bfloat16)


def draw_text_tokens(key, part):
    return feature_tokens(jax.random.fold_in(key, 21), (2, PROMPTS, TXT, D))


def draw_image_tokens(key, part):
    return feature_tokens(jax.random.fold_in(key, 22), (PROMPTS, IMG, D))


def steps_of(key, dims, cuts, smallest, top_value):
    def one(dim, shards_of):
        draws = jax.random.uniform(jax.random.fold_in(jax.random.fold_in(key, 6), dim), (shards_of,), jnp.float32, smallest / len(cuts), top_value / len(cuts))
        return jnp.repeat(jnp.exp(draws), dims[dim] // shards_of).reshape((-1,) + (1,) * (len(dims) - dim - 1))

    factor_of = one(*cuts[0])
    for cut in cuts[1:]:
        factor_of = factor_of * one(*cut)
    return factor_of


def centred(own_key, dims, deviation, bound, pieces=(), kind=jnp.bfloat16):
    result = jax.random.normal(own_key, dims, jnp.float32) * deviation
    if len(pieces) > 0:
        result = steps_of(own_key, dims, pieces, -0.22, 0.18) * result
    return jnp.clip(result, min=-bound, max=bound).astype(kind)


def setup_inputs(seed: int = 0) -> dict:
    arg_keys = jax.random.split(jax.random.key(seed), 13)
    text_tokens = draw_text_tokens(jax.random.fold_in(arg_keys[12], 71), 0)
    image_tokens = draw_image_tokens(jax.random.fold_in(arg_keys[12], 71), 0)
    pooled_vector = centred(arg_keys[2], (2, D), 1.0, 6.0, ((0, 2), (1, 16)), jnp.float32)
    mod_weight = centred(arg_keys[3], (D, 3, D), D ** -0.5, 0.109375, ((0, 16), (2, 8)))
    qkv_weight = centred(arg_keys[4], (D, 3, HEADS, HD), D ** -0.5, 0.109375, ((0, 16), (2, 8)))
    up_weight = centred(arg_keys[5], (D, MLP), D ** -0.5, 0.109375, ((0, 16), (1, 8)))
    query_gain = draw_query_gain(jax.random.fold_in(arg_keys[12], 71), 0)
    key_gain = draw_key_gain(jax.random.fold_in(arg_keys[12], 71), 0)
    attn_weight = centred(arg_keys[8], (HEADS * HD, D), (HEADS * HD) ** -0.5, 0.125, ((0, 8), (1, 16)))
    down_weight = centred(arg_keys[9], (MLP, D), MLP ** -0.5, 0.078125, ((0, 8), (1, 16)))
    lengths = draw_lengths(jax.random.fold_in(arg_keys[12], 71), 0)
    timestep = jax.random.randint(arg_keys[11], (1,), 0, STEPS).astype(jnp.int32)
    return dict(text_tokens=text_tokens, image_tokens=image_tokens, pooled_vector=pooled_vector, mod_weight=mod_weight, qkv_weight=qkv_weight, up_weight=up_weight, query_gain=query_gain, key_gain=key_gain, attn_weight=attn_weight, down_weight=down_weight, lengths=lengths, timestep=timestep)


epsilon = 1e-06
guidance = 3.5
time_shift = 3.0
rope_theta = 10000.0

def plan(timestep):
    step_index = timestep[0].astype(jnp.float32)
    time_now = 1.0 - step_index / STEPS
    time_next = 1.0 - (step_index + 1.0) / STEPS
    sigma_now = time_shift * time_now / (1.0 + (time_shift - 1.0) * time_now)
    sigma_next = time_shift * time_next / (1.0 + (time_shift - 1.0) * time_next)
    return (sigma_now, sigma_next - sigma_now)

def time_embedding(sigma_now, dim_count):
    halfwidth = dim_count // 2
    frequency = jnp.exp(-math.log(10000.0) * jnp.arange(halfwidth, dtype=jnp.float32) / halfwidth)
    angles = 1000.0 * sigma_now * frequency
    return jnp.concatenate([jnp.cos(angles), jnp.sin(angles)])

def inverse_freq(dim_count):
    return rope_theta ** (-jnp.arange(0, dim_count, 2, dtype=jnp.float32) / dim_count)

def rotary_angles(height_pos, width_pos):
    still_dims = HD // 8
    axis_dims = (HD - still_dims) // 2
    return jnp.concatenate([jnp.zeros((height_pos.shape[0], still_dims // 2), jnp.float32), height_pos[:, None] * inverse_freq(axis_dims)[None], width_pos[:, None] * inverse_freq(axis_dims)[None]], axis=1)

def rotate(vectors, angles):
    paired_dims = vectors.reshape(vectors.shape[:-1] + (HD // 2, 2))
    cosine_table = jnp.cos(angles)[:, None, :]
    sine_table = jnp.sin(angles)[:, None, :]
    first_part = paired_dims[..., 0]
    second_part = paired_dims[..., 1]
    turned = jnp.stack([first_part * cosine_table - second_part * sine_table, first_part * sine_table + second_part * cosine_table], axis=-1)
    return turned.reshape(vectors.shape)

def head_norm(vectors, gain_vector):
    return vectors * lax.rsqrt(lax.optimization_barrier(jnp.mean(vectors * vectors, axis=-1, keepdims=True)) + epsilon) * gain_vector

def layer(tokens, modulation, qkv_weight, up_weight, query_gain, key_gain, attn_weight, down_weight, length, angles):
    seq_len = TXT + IMG
    hidden = tokens.astype(jnp.float32)
    average = lax.optimization_barrier(jnp.mean(hidden, axis=-1, keepdims=True))
    variance = lax.optimization_barrier(jnp.mean(hidden * hidden, axis=-1, keepdims=True)) - average * average
    normed = ((hidden - average) * lax.rsqrt(variance + epsilon) * (1.0 + modulation[1]) + modulation[0]).astype(jnp.bfloat16)
    projected = jnp.dot(normed, qkv_weight.reshape(D, 3 * HEADS * HD), preferred_element_type=jnp.float32)
    projected = projected.reshape(seq_len, 3, HEADS, HD)
    mlp_units = jnp.dot(normed, up_weight, preferred_element_type=jnp.float32)
    queries = rotate(head_norm(projected[:, 0], query_gain), angles).astype(jnp.bfloat16)
    key_rows = rotate(head_norm(projected[:, 1], key_gain), angles).astype(jnp.bfloat16)
    values = projected[:, 2].astype(jnp.bfloat16)
    positions = jnp.arange(seq_len, dtype=jnp.int32)
    key_live = (positions >= TXT) | (positions < length)

    def one_head(head_index):
        query_head = lax.dynamic_index_in_dim(queries, head_index, 1, keepdims=False)
        key_head = lax.dynamic_index_in_dim(key_rows, head_index, 1, keepdims=False)
        value_head = lax.dynamic_index_in_dim(values, head_index, 1, keepdims=False)
        scores = jnp.dot(query_head, key_head.T, preferred_element_type=jnp.float32) * HD ** (-0.5)
        scores = jnp.where(key_live[None, :], scores, -1e+30)
        top_score = lax.optimization_barrier(jnp.max(scores, axis=-1, keepdims=True))
        weights = jnp.exp(scores - top_score)
        denominator = lax.optimization_barrier(jnp.sum(weights, axis=-1, keepdims=True))
        mixed = jnp.dot(weights.astype(jnp.bfloat16), value_head, preferred_element_type=jnp.float32)
        return (mixed / denominator).astype(jnp.bfloat16)
    attended = lax.map(one_head, jnp.arange(HEADS, dtype=jnp.int32))
    attended = attended.transpose(1, 0, 2).reshape(seq_len, HEADS * HD)
    activated = jax.nn.gelu(mlp_units, approximate=True).astype(jnp.bfloat16)
    head_block = HEADS // N_WBLK * HD
    unit_block = MLP // N_WBLK
    branch = jnp.zeros((seq_len, D), jnp.float32)
    for block_index in range(N_WBLK):
        block_term = jnp.dot(attended[:, block_index * head_block:(block_index + 1) * head_block], attn_weight[block_index * head_block:(block_index + 1) * head_block], preferred_element_type=jnp.float32)
        block_term = block_term + jnp.dot(activated[:, block_index * unit_block:(block_index + 1) * unit_block], down_weight[block_index * unit_block:(block_index + 1) * unit_block], preferred_element_type=jnp.float32)
        rounded = lax.optimization_barrier(block_term.astype(jnp.bfloat16))
        branch = branch + rounded.astype(jnp.float32)
    return hidden + modulation[2] * branch

def reference(text_tokens, image_tokens, pooled_vector, mod_weight, qkv_weight, up_weight, query_gain, key_gain, attn_weight, down_weight, lengths, timestep):
    sigma_now, step_size = plan(timestep)
    cond_vec = jax.nn.silu(pooled_vector + time_embedding(sigma_now, D)[None]).astype(jnp.bfloat16)
    modulation = jnp.dot(cond_vec, mod_weight.reshape(D, 3 * D), preferred_element_type=jnp.float32).reshape(2, 3, D)
    image_index = jnp.arange(IMG, dtype=jnp.int32)
    height_pos = jnp.concatenate([jnp.zeros((TXT,), jnp.float32), (image_index // GRID).astype(jnp.float32)])
    width_pos = jnp.concatenate([jnp.zeros((TXT,), jnp.float32), (image_index % GRID).astype(jnp.float32)])
    angles = rotary_angles(height_pos, width_pos)
    text_halves = []
    image_halves = []
    for half_index in range(2):
        text_list = []
        image_list = []
        for prompt in range(PROMPTS):
            tokens = jnp.concatenate([text_tokens[half_index, prompt], image_tokens[prompt]], axis=0)
            layer_out = layer(tokens, modulation[half_index], qkv_weight, up_weight, query_gain, key_gain, attn_weight, down_weight, lengths[prompt], angles)
            text_list.append(layer_out[:TXT].astype(jnp.bfloat16))
            image_list.append(layer_out[TXT:])
        text_halves.append(jnp.stack(text_list))
        image_halves.append(jnp.stack(image_list))
    text_out = jnp.stack(text_halves)
    velocity = image_halves[1] + guidance * (image_halves[0] - image_halves[1])
    new_image = image_tokens.astype(jnp.float32) + step_size * velocity
    return (text_out, velocity, new_image)
```

```python
import math

import jax
import jax.numpy as jnp
from jax import lax
from jax.sharding import PartitionSpec as P

D = 3072
HD = 128
GRID = 64
STEPS = 28


epsilon = 1e-06
guidance = 3.5
time_shift = 3.0
rope_theta = 10000.0


def plan(timestep):
    step_index = timestep[0].astype(jnp.float32)
    time_now = 1.0 - step_index / STEPS
    time_next = 1.0 - (step_index + 1.0) / STEPS
    sigma_now = time_shift * time_now / (1.0 + (time_shift - 1.0) * time_now)
    sigma_next = time_shift * time_next / (1.0 + (time_shift - 1.0) * time_next)
    return (sigma_now, sigma_next - sigma_now)


def time_embedding(sigma_now, dim_count):
    halfwidth = dim_count // 2
    frequency = jnp.exp(-math.log(10000.0) * jnp.arange(halfwidth, dtype=jnp.float32) / halfwidth)
    angles = 1000.0 * sigma_now * frequency
    return jnp.concatenate([jnp.cos(angles), jnp.sin(angles)])


def inverse_freq(dim_count):
    return rope_theta ** (-jnp.arange(0, dim_count, 2, dtype=jnp.float32) / dim_count)


def rotary_angles(height_pos, width_pos):
    still_dims = HD // 8
    axis_dims = (HD - still_dims) // 2
    return jnp.concatenate(
        [
            jnp.zeros((height_pos.shape[0], still_dims // 2), jnp.float32),
            height_pos[:, None] * inverse_freq(axis_dims)[None],
            width_pos[:, None] * inverse_freq(axis_dims)[None],
        ],
        axis=1,
    )


def rotate(vectors, angles):
    paired_dims = vectors.reshape(vectors.shape[:-1] + (HD // 2, 2))
    cosine_table = jnp.cos(angles)[:, None, :]
    sine_table = jnp.sin(angles)[:, None, :]
    first_part = paired_dims[..., 0]
    second_part = paired_dims[..., 1]
    turned = jnp.stack(
        [
            first_part * cosine_table - second_part * sine_table,
            first_part * sine_table + second_part * cosine_table,
        ],
        axis=-1,
    )
    return turned.reshape(vectors.shape)


def head_norm(vectors, gain_vector):
    return (
        vectors
        * lax.rsqrt(jnp.mean(vectors * vectors, axis=-1, keepdims=True) + epsilon)
        * gain_vector
    )


def input_folder(source, pieces):
    width_rows = pieces[0].shape[0]
    first_total = jnp.dot(
        source, pieces[0].reshape(width_rows, -1), preferred_element_type=jnp.float32
    )
    second_total = jnp.dot(source, pieces[1], preferred_element_type=jnp.float32)
    return (first_total, second_total)


def output_folder(attended, activated, pieces):
    block_cols = jnp.dot(attended, pieces[0], preferred_element_type=jnp.float32)
    block_cols = block_cols + jnp.dot(activated, pieces[1], preferred_element_type=jnp.float32)
    return block_cols


def shards(
    text_tokens,
    image_tokens,
    pooled_vector,
    mod_weight,
    qkv_weight,
    up_weight,
    query_gain,
    key_gain,
    attn_weight,
    down_weight,
    lengths,
    timestep,
):
    seq_pos = lax.axis_index("seq")
    cfg_pos = lax.axis_index("cfg")
    prompts = image_tokens.shape[0]
    image_rows = image_tokens.shape[1]
    text_rows = text_tokens.shape[2]
    local_len = text_rows + image_rows
    dim_local = image_tokens.shape[2]
    dim_seq = pooled_vector.shape[1]
    heads_local = qkv_weight.shape[2]
    row_count = prompts * local_len
    sigma_now, step_size = plan(timestep)
    embedded = lax.dynamic_slice_in_dim(time_embedding(sigma_now, D), seq_pos * dim_seq, dim_seq)
    cond_vec = jax.nn.silu(pooled_vector[0] + embedded).astype(jnp.bfloat16)[None]
    mod_terms = jnp.dot(
        cond_vec, mod_weight.reshape(dim_seq, 3 * dim_local), preferred_element_type=jnp.float32
    )
    modulation = lax.psum(mod_terms.reshape(3, dim_local), "seq")
    local_rows = jnp.concatenate([text_tokens[0], image_tokens], axis=1)
    hidden = local_rows.astype(jnp.float32)
    totals, squares = lax.psum(
        (jnp.sum(hidden, axis=-1), jnp.sum(hidden * hidden, axis=-1)), "wblk"
    )
    average = (totals / D)[..., None]
    variance = (squares / D)[..., None] - average * average
    normed = (
        (hidden - average) * lax.rsqrt(variance + epsilon) * (1.0 + modulation[1]) + modulation[0]
    ).astype(jnp.bfloat16)
    gathered = lax.all_gather(normed, "wblk", axis=2, tiled=True)
    token_rows = gathered.reshape(row_count, D)
    projected, mlp_units = input_folder(
        token_rows,
        (
            lax.all_gather(qkv_weight, "seq", axis=0, tiled=True),
            lax.all_gather(up_weight, "seq", axis=0, tiled=True),
        ),
    )
    projected = projected.reshape(prompts, local_len, 3, heads_local, HD)
    image_index = seq_pos * image_rows + jnp.arange(image_rows, dtype=jnp.int32)
    height_pos = jnp.concatenate(
        [jnp.zeros((text_rows,), jnp.float32), (image_index // GRID).astype(jnp.float32)]
    )
    width_pos = jnp.concatenate(
        [jnp.zeros((text_rows,), jnp.float32), (image_index % GRID).astype(jnp.float32)]
    )
    angles = rotary_angles(height_pos, width_pos)
    queries = rotate(head_norm(projected[:, :, 0], query_gain), angles).astype(jnp.bfloat16)
    key_rows = rotate(head_norm(projected[:, :, 1], key_gain), angles).astype(jnp.bfloat16)
    values = projected[:, :, 2].astype(jnp.bfloat16)
    scale_factor = HD ** (-0.5)
    seq_count = lax.psum(1, "seq")
    pair_count = prompts * heads_local
    subs = seq_count // pair_count
    sub_rows = local_len // subs
    pair_keys = key_rows.transpose(0, 2, 1, 3).reshape(pair_count, local_len, HD)
    pair_values = values.transpose(0, 2, 1, 3).reshape(pair_count, local_len, HD)
    pair_queries = queries.transpose(0, 2, 1, 3).reshape(seq_count, sub_rows, HD)
    send = jnp.concatenate(
        [
            jnp.broadcast_to(pair_keys[:, None], (pair_count, subs, local_len, HD)).reshape(
                seq_count, local_len, HD
            ),
            jnp.broadcast_to(pair_values[:, None], (pair_count, subs, local_len, HD)).reshape(
                seq_count, local_len, HD
            ),
            pair_queries,
        ],
        axis=1,
    )
    received = lax.all_to_all(send, "seq", 0, 0, tiled=True)
    key_piece = received[:, :local_len].reshape(seq_count * local_len, HD)
    value_piece = received[:, local_len : 2 * local_len].reshape(seq_count * local_len, HD)
    query_piece = received[:, 2 * local_len :].reshape(seq_count * sub_rows, HD)
    my_prompt = seq_pos // subs // heads_local
    width_keys = key_piece.shape[0]
    where_global = jnp.arange(width_keys, dtype=jnp.int32)
    shard_index = where_global // local_len
    within = where_global % local_len
    text_index = shard_index * text_rows + within
    key_live = (within >= text_rows) | (text_index < lengths[my_prompt])
    scores = (
        jnp.dot(query_piece, key_piece.T, preferred_element_type=jnp.float32) * scale_factor
    )
    scores = jnp.where(key_live[None, :], scores, -1e30)
    top_score = jnp.max(scores, axis=-1, keepdims=True)
    weights = jnp.exp(scores - top_score)
    denominator = jnp.sum(weights, axis=-1, keepdims=True)
    numerator = jnp.dot(
        weights.astype(jnp.bfloat16), value_piece, preferred_element_type=jnp.float32
    )
    mixed = (numerator / denominator).astype(jnp.bfloat16).reshape(seq_count, sub_rows, HD)
    returned = lax.all_to_all(mixed, "seq", 0, 0, tiled=True)
    attended = returned.reshape(prompts, heads_local, local_len, HD)
    attended = attended.transpose(0, 2, 1, 3).reshape(row_count, heads_local * HD)
    activated = jax.nn.gelu(mlp_units, approximate=True).astype(jnp.bfloat16)
    branch_terms = output_folder(
        attended,
        activated,
        (
            lax.all_gather(attn_weight, "seq", axis=1, tiled=True),
            lax.all_gather(down_weight, "seq", axis=1, tiled=True),
        ),
    )
    branch = lax.psum_scatter(
        branch_terms.reshape(prompts, local_len, D).astype(jnp.bfloat16),
        "wblk",
        scatter_dimension=2,
        tiled=True,
    ).astype(jnp.float32)
    layer_out = hidden + modulation[2] * branch
    text_out = layer_out[:, :text_rows].astype(jnp.bfloat16)[None]
    image_out = layer_out[:, text_rows:]
    paired = lax.all_to_all(
        image_out[:, None].astype(jnp.bfloat16), "cfg", split_axis=0, concat_axis=1, tiled=True
    ).astype(jnp.float32)
    velocity = paired[:, 1] + guidance * (paired[:, 0] - paired[:, 1])
    own_prompts = prompts // 2
    latent = lax.dynamic_slice_in_dim(image_tokens, cfg_pos * own_prompts, own_prompts, 0).astype(
        jnp.float32
    )
    new_image = latent + step_size * velocity
    return (text_out, velocity, new_image)


def solution(mesh):
    in_specs = (
        P("cfg", None, "seq", "wblk"),
        P(None, "seq", "wblk"),
        P("cfg", "seq"),
        P("seq", None, "wblk"),
        P("seq", None, "wblk", None),
        P("seq", "wblk"),
        P(),
        P(),
        P("wblk", "seq"),
        P("wblk", "seq"),
        P(),
        P(),
    )
    out_specs = (P("cfg", None, "seq", "wblk"), P("cfg", "seq", "wblk"), P("cfg", "seq", "wblk"))
    return jax.shard_map(shards, mesh=mesh, in_specs=in_specs, out_specs=out_specs, check_vma=False)
```

```python
import math

import jax
import jax.numpy as jnp
from jax import lax
from jax.sharding import PartitionSpec as P

D = 3072
HD = 128
GRID = 64
STEPS = 28


epsilon = 1e-06
guidance = 3.5
time_shift = 3.0
rope_theta = 10000.0


def plan(timestep):
    step_index = timestep[0].astype(jnp.float32)
    time_now = 1.0 - step_index / STEPS
    time_next = 1.0 - (step_index + 1.0) / STEPS
    sigma_now = time_shift * time_now / (1.0 + (time_shift - 1.0) * time_now)
    sigma_next = time_shift * time_next / (1.0 + (time_shift - 1.0) * time_next)
    return (sigma_now, sigma_next - sigma_now)


def time_embedding(sigma_now, dim_count):
    halfwidth = dim_count // 2
    frequency = jnp.exp(-math.log(10000.0) * jnp.arange(halfwidth, dtype=jnp.float32) / halfwidth)
    angles = 1000.0 * sigma_now * frequency
    return jnp.concatenate([jnp.cos(angles), jnp.sin(angles)])


def inverse_freq(dim_count):
    return rope_theta ** (-jnp.arange(0, dim_count, 2, dtype=jnp.float32) / dim_count)


def rotary_angles(height_pos, width_pos):
    still_dims = HD // 8
    axis_dims = (HD - still_dims) // 2
    return jnp.concatenate(
        [
            jnp.zeros((height_pos.shape[0], still_dims // 2), jnp.float32),
            height_pos[:, None] * inverse_freq(axis_dims)[None],
            width_pos[:, None] * inverse_freq(axis_dims)[None],
        ],
        axis=1,
    )


def rotate(vectors, angles):
    paired_dims = vectors.reshape(vectors.shape[:-1] + (HD // 2, 2))
    cosine_table = jnp.cos(angles)[:, None, :]
    sine_table = jnp.sin(angles)[:, None, :]
    first_part = paired_dims[..., 0]
    second_part = paired_dims[..., 1]
    turned = jnp.stack(
        [
            first_part * cosine_table - second_part * sine_table,
            first_part * sine_table + second_part * cosine_table,
        ],
        axis=-1,
    )
    return turned.reshape(vectors.shape)


def head_norm(vectors, gain_vector):
    return (
        vectors
        * lax.rsqrt(jnp.mean(vectors * vectors, axis=-1, keepdims=True) + epsilon)
        * gain_vector
    )


def input_folder(source, pieces):
    width_rows = pieces[0].shape[0]
    first_total = jnp.dot(
        source, pieces[0].reshape(width_rows, -1), preferred_element_type=jnp.float32
    )
    second_total = jnp.dot(source, pieces[1], preferred_element_type=jnp.float32)
    return (first_total, second_total)


def output_folder(attended, activated, pieces):
    block_cols = jnp.dot(attended, pieces[0], preferred_element_type=jnp.float32)
    block_cols = block_cols + jnp.dot(activated, pieces[1], preferred_element_type=jnp.float32)
    return block_cols


def shards(
    text_tokens,
    image_tokens,
    pooled_vector,
    mod_weight,
    qkv_weight,
    up_weight,
    query_gain,
    key_gain,
    attn_weight,
    down_weight,
    lengths,
    timestep,
):
    seq_pos = lax.axis_index("seq")
    cfg_pos = lax.axis_index("cfg")
    prompts = image_tokens.shape[0]
    image_rows = image_tokens.shape[1]
    text_rows = text_tokens.shape[2]
    local_len = text_rows + image_rows
    dim_local = image_tokens.shape[2]
    dim_seq = pooled_vector.shape[1]
    heads_local = qkv_weight.shape[2]
    row_count = prompts * local_len
    sigma_now, step_size = plan(timestep)
    embedded = lax.dynamic_slice_in_dim(time_embedding(sigma_now, D), seq_pos * dim_seq, dim_seq)
    cond_vec = jax.nn.silu(pooled_vector[0] + embedded).astype(jnp.bfloat16)[None]
    mod_terms = jnp.dot(
        cond_vec, mod_weight.reshape(dim_seq, 3 * dim_local), preferred_element_type=jnp.float32
    )
    modulation = lax.psum(mod_terms.reshape(3, dim_local), "seq")
    local_rows = jnp.concatenate([text_tokens[0], image_tokens], axis=1)
    hidden = local_rows.astype(jnp.float32)
    totals, squares = lax.psum(
        (jnp.sum(hidden, axis=-1), jnp.sum(hidden * hidden, axis=-1)), "wblk"
    )
    average = (totals / D)[..., None]
    variance = (squares / D)[..., None] - average * average
    normed = (
        (hidden - average) * lax.rsqrt(variance + epsilon) * (1.0 + modulation[1]) + modulation[0]
    ).astype(jnp.bfloat16)
    width_rows = qkv_weight.shape[0]
    qkv_cols = 3 * heads_local * HD
    in_weight = lax.all_gather(
        jnp.concatenate([qkv_weight.reshape(width_rows, qkv_cols), up_weight], axis=1),
        "seq",
        axis=0,
        tiled=True,
    )
    normed, in_weight = lax.optimization_barrier((normed, in_weight))
    gathered = lax.all_gather(normed, "wblk", axis=2, tiled=True)
    token_rows = gathered.reshape(row_count, D)
    both = jnp.dot(token_rows, in_weight, preferred_element_type=jnp.float32)
    projected = both[:, :qkv_cols]
    mlp_units = both[:, qkv_cols:]
    projected = projected.reshape(prompts, local_len, 3, heads_local, HD)
    image_index = seq_pos * image_rows + jnp.arange(image_rows, dtype=jnp.int32)
    height_pos = jnp.concatenate(
        [jnp.zeros((text_rows,), jnp.float32), (image_index // GRID).astype(jnp.float32)]
    )
    width_pos = jnp.concatenate(
        [jnp.zeros((text_rows,), jnp.float32), (image_index % GRID).astype(jnp.float32)]
    )
    angles = rotary_angles(height_pos, width_pos)
    queries = rotate(head_norm(projected[:, :, 0], query_gain), angles).astype(jnp.bfloat16)
    key_rows = rotate(head_norm(projected[:, :, 1], key_gain), angles).astype(jnp.bfloat16)
    values = projected[:, :, 2].astype(jnp.bfloat16)
    scale_factor = HD ** (-0.5)
    seq_count = lax.psum(1, "seq")
    pair_count = prompts * heads_local
    subs = seq_count // pair_count
    sub_rows = local_len // subs
    pair_keys = key_rows.transpose(0, 2, 1, 3).reshape(pair_count, local_len, HD)
    pair_values = values.transpose(0, 2, 1, 3).reshape(pair_count, local_len, HD)
    pair_queries = queries.transpose(0, 2, 1, 3).reshape(seq_count, sub_rows, HD)
    send = jnp.concatenate(
        [
            jnp.broadcast_to(pair_keys[:, None], (pair_count, subs, local_len, HD)).reshape(
                seq_count, local_len, HD
            ),
            jnp.broadcast_to(pair_values[:, None], (pair_count, subs, local_len, HD)).reshape(
                seq_count, local_len, HD
            ),
            pair_queries,
        ],
        axis=1,
    )
    received = lax.all_to_all(send, "seq", 0, 0, tiled=True)
    key_piece = received[:, :local_len].reshape(seq_count * local_len, HD)
    value_piece = received[:, local_len : 2 * local_len].reshape(seq_count * local_len, HD)
    query_piece = received[:, 2 * local_len :].reshape(seq_count * sub_rows, HD)
    my_prompt = seq_pos // subs // heads_local
    width_keys = key_piece.shape[0]
    where_global = jnp.arange(width_keys, dtype=jnp.int32)
    shard_index = where_global // local_len
    within = where_global % local_len
    text_index = shard_index * text_rows + within
    key_live = (within >= text_rows) | (text_index < lengths[my_prompt])
    scores = (
        jnp.dot(query_piece, key_piece.T, preferred_element_type=jnp.float32) * scale_factor
    )
    scores = jnp.where(key_live[None, :], scores, -1e30)
    top_score = jnp.max(scores, axis=-1, keepdims=True)
    weights = jnp.exp(scores - top_score)
    denominator = jnp.sum(weights, axis=-1, keepdims=True)
    numerator = jnp.dot(
        weights.astype(jnp.bfloat16), value_piece, preferred_element_type=jnp.float32
    )
    mixed = (numerator / denominator).astype(jnp.bfloat16).reshape(seq_count, sub_rows, HD)
    returned = lax.all_to_all(mixed, "seq", 0, 0, tiled=True)
    attended = returned.reshape(prompts, heads_local, local_len, HD)
    attended = attended.transpose(0, 2, 1, 3).reshape(row_count, heads_local * HD)
    activated = jax.nn.gelu(mlp_units, approximate=True).astype(jnp.bfloat16)
    out_weight = lax.all_gather(
        jnp.concatenate([attn_weight, down_weight], axis=0), "seq", axis=1, tiled=True
    )
    branch_terms = jnp.dot(
        jnp.concatenate([attended, activated], axis=1),
        out_weight,
        preferred_element_type=jnp.float32,
    )
    branch = lax.psum_scatter(
        branch_terms.reshape(prompts, local_len, D).astype(jnp.bfloat16),
        "wblk",
        scatter_dimension=2,
        tiled=True,
    ).astype(jnp.float32)
    layer_out = hidden + modulation[2] * branch
    text_out = layer_out[:, :text_rows].astype(jnp.bfloat16)[None]
    image_out = layer_out[:, text_rows:]
    paired = lax.all_to_all(
        image_out[:, None].astype(jnp.bfloat16), "cfg", split_axis=0, concat_axis=1, tiled=True
    ).astype(jnp.float32)
    velocity = paired[:, 1] + guidance * (paired[:, 0] - paired[:, 1])
    own_prompts = prompts // 2
    latent = lax.dynamic_slice_in_dim(image_tokens, cfg_pos * own_prompts, own_prompts, 0).astype(
        jnp.float32
    )
    new_image = latent + step_size * velocity
    return (text_out, velocity, new_image)


def solution(mesh):
    in_specs = (
        P("cfg", None, "seq", "wblk"),
        P(None, "seq", "wblk"),
        P("cfg", "seq"),
        P("seq", None, "wblk"),
        P("seq", None, "wblk", None),
        P("seq", "wblk"),
        P(),
        P(),
        P("wblk", "seq"),
        P("wblk", "seq"),
        P(),
        P(),
    )
    out_specs = (P("cfg", None, "seq", "wblk"), P("cfg", "seq", "wblk"), P("cfg", "seq", "wblk"))
    return jax.shard_map(shards, mesh=mesh, in_specs=in_specs, out_specs=out_specs, check_vma=False)
```

```python
import math

import jax
import jax.numpy as jnp
from jax import lax
from jax.sharding import PartitionSpec as P

D = 3072
HD = 128
GRID = 64
STEPS = 28


epsilon = 1e-06
guidance = 3.5
time_shift = 3.0
rope_theta = 10000.0


def plan(timestep):
    step_index = timestep[0].astype(jnp.float32)
    time_now = 1.0 - step_index / STEPS
    time_next = 1.0 - (step_index + 1.0) / STEPS
    sigma_now = time_shift * time_now / (1.0 + (time_shift - 1.0) * time_now)
    sigma_next = time_shift * time_next / (1.0 + (time_shift - 1.0) * time_next)
    return (sigma_now, sigma_next - sigma_now)


def time_embedding(sigma_now, dim_count):
    halfwidth = dim_count // 2
    frequency = jnp.exp(-math.log(10000.0) * jnp.arange(halfwidth, dtype=jnp.float32) / halfwidth)
    angles = 1000.0 * sigma_now * frequency
    return jnp.concatenate([jnp.cos(angles), jnp.sin(angles)])


def inverse_freq(dim_count):
    return rope_theta ** (-jnp.arange(0, dim_count, 2, dtype=jnp.float32) / dim_count)


def rotary_angles(height_pos, width_pos):
    still_dims = HD // 8
    axis_dims = (HD - still_dims) // 2
    return jnp.concatenate(
        [
            jnp.zeros((height_pos.shape[0], still_dims // 2), jnp.float32),
            height_pos[:, None] * inverse_freq(axis_dims)[None],
            width_pos[:, None] * inverse_freq(axis_dims)[None],
        ],
        axis=1,
    )


def rotate(vectors, angles):
    paired_dims = vectors.reshape(vectors.shape[:-1] + (HD // 2, 2))
    cosine_table = jnp.cos(angles)[:, None, :]
    sine_table = jnp.sin(angles)[:, None, :]
    first_part = paired_dims[..., 0]
    second_part = paired_dims[..., 1]
    turned = jnp.stack(
        [
            first_part * cosine_table - second_part * sine_table,
            first_part * sine_table + second_part * cosine_table,
        ],
        axis=-1,
    )
    return turned.reshape(vectors.shape)


def head_norm(vectors, gain_vector):
    return (
        vectors
        * lax.rsqrt(jnp.mean(vectors * vectors, axis=-1, keepdims=True) + epsilon)
        * gain_vector
    )


def input_folder(source, pieces):
    width_rows = pieces[0].shape[0]
    first_total = jnp.dot(
        source, pieces[0].reshape(width_rows, -1), preferred_element_type=jnp.float32
    )
    second_total = jnp.dot(source, pieces[1], preferred_element_type=jnp.float32)
    return (first_total, second_total)


def output_folder(attended, activated, pieces):
    block_cols = jnp.dot(attended, pieces[0], preferred_element_type=jnp.float32)
    block_cols = block_cols + jnp.dot(activated, pieces[1], preferred_element_type=jnp.float32)
    return block_cols


def shards(
    text_tokens,
    image_tokens,
    pooled_vector,
    mod_weight,
    qkv_weight,
    up_weight,
    query_gain,
    key_gain,
    attn_weight,
    down_weight,
    lengths,
    timestep,
):
    seq_pos = lax.axis_index("seq")
    cfg_pos = lax.axis_index("cfg")
    prompts = image_tokens.shape[0]
    image_rows = image_tokens.shape[1]
    text_rows = text_tokens.shape[2]
    local_len = text_rows + image_rows
    dim_local = image_tokens.shape[2]
    dim_seq = pooled_vector.shape[1]
    heads_local = qkv_weight.shape[2]
    row_count = prompts * local_len
    sigma_now, step_size = plan(timestep)
    embedded = lax.dynamic_slice_in_dim(time_embedding(sigma_now, D), seq_pos * dim_seq, dim_seq)
    cond_vec = jax.nn.silu(pooled_vector[0] + embedded).astype(jnp.bfloat16)[None]
    mod_terms = jnp.dot(
        cond_vec, mod_weight.reshape(dim_seq, 3 * dim_local), preferred_element_type=jnp.float32
    )
    modulation = lax.psum(mod_terms.reshape(3, dim_local), "seq")
    local_rows = jnp.concatenate([text_tokens[0], image_tokens], axis=1)
    hidden = local_rows.astype(jnp.float32)
    totals, squares = lax.psum(
        (jnp.sum(hidden, axis=-1), jnp.sum(hidden * hidden, axis=-1)), "wblk"
    )
    average = (totals / D)[..., None]
    variance = (squares / D)[..., None] - average * average
    normed = (
        (hidden - average) * lax.rsqrt(variance + epsilon) * (1.0 + modulation[1]) + modulation[0]
    ).astype(jnp.bfloat16)
    width_rows = qkv_weight.shape[0]
    qkv_cols = 3 * heads_local * HD
    in_weight = lax.all_gather(
        jnp.concatenate([qkv_weight.reshape(width_rows, qkv_cols), up_weight], axis=1),
        "seq",
        axis=0,
        tiled=True,
    )
    wblk_count = lax.psum(1, "wblk")
    spread = jnp.broadcast_to(normed.reshape(1, row_count, dim_local), (wblk_count, row_count, dim_local))
    gathered = lax.all_to_all(spread, "wblk", 0, 0, tiled=True)
    both = jnp.einsum(
        "wrf,wfn->rn",
        gathered,
        in_weight.reshape(wblk_count, dim_local, -1),
        preferred_element_type=jnp.float32,
    )
    projected = both[:, :qkv_cols]
    mlp_units = both[:, qkv_cols:]
    projected = projected.reshape(prompts, local_len, 3, heads_local, HD)
    image_index = seq_pos * image_rows + jnp.arange(image_rows, dtype=jnp.int32)
    height_pos = jnp.concatenate(
        [jnp.zeros((text_rows,), jnp.float32), (image_index // GRID).astype(jnp.float32)]
    )
    width_pos = jnp.concatenate(
        [jnp.zeros((text_rows,), jnp.float32), (image_index % GRID).astype(jnp.float32)]
    )
    angles = rotary_angles(height_pos, width_pos)
    queries = rotate(head_norm(projected[:, :, 0], query_gain), angles).astype(jnp.bfloat16)
    key_rows = rotate(head_norm(projected[:, :, 1], key_gain), angles).astype(jnp.bfloat16)
    values = projected[:, :, 2].astype(jnp.bfloat16)
    scale_factor = HD ** (-0.5)
    seq_count = lax.psum(1, "seq")
    pair_count = prompts * heads_local
    subs = seq_count // pair_count
    sub_rows = local_len // subs
    pair_keys = key_rows.transpose(0, 2, 1, 3).reshape(pair_count, local_len, HD)
    pair_values = values.transpose(0, 2, 1, 3).reshape(pair_count, local_len, HD)
    pair_queries = queries.transpose(0, 2, 1, 3).reshape(seq_count, sub_rows, HD)
    send = jnp.concatenate(
        [
            jnp.broadcast_to(pair_keys[:, None], (pair_count, subs, local_len, HD)).reshape(
                seq_count, local_len, HD
            ),
            jnp.broadcast_to(pair_values[:, None], (pair_count, subs, local_len, HD)).reshape(
                seq_count, local_len, HD
            ),
            pair_queries,
        ],
        axis=1,
    )
    received = lax.all_to_all(send, "seq", 0, 0, tiled=True)
    key_piece = received[:, :local_len].reshape(seq_count * local_len, HD)
    value_piece = received[:, local_len : 2 * local_len].reshape(seq_count * local_len, HD)
    query_piece = received[:, 2 * local_len :].reshape(seq_count * sub_rows, HD)
    my_prompt = seq_pos // subs // heads_local
    width_keys = key_piece.shape[0]
    where_global = jnp.arange(width_keys, dtype=jnp.int32)
    shard_index = where_global // local_len
    within = where_global % local_len
    text_index = shard_index * text_rows + within
    key_live = (within >= text_rows) | (text_index < lengths[my_prompt])
    scores = (
        jnp.dot(query_piece, key_piece.T, preferred_element_type=jnp.float32) * scale_factor
    )
    scores = jnp.where(key_live[None, :], scores, -1e30)
    top_score = jnp.max(scores, axis=-1, keepdims=True)
    weights = jnp.exp(scores - top_score)
    denominator = jnp.sum(weights, axis=-1, keepdims=True)
    numerator = jnp.dot(
        weights.astype(jnp.bfloat16), value_piece, preferred_element_type=jnp.float32
    )
    mixed = (numerator / denominator).astype(jnp.bfloat16).reshape(seq_count, sub_rows, HD)
    returned = lax.all_to_all(mixed, "seq", 0, 0, tiled=True)
    attended = returned.reshape(prompts, heads_local, local_len, HD)
    attended = attended.transpose(0, 2, 1, 3).reshape(row_count, heads_local * HD)
    activated = jax.nn.gelu(mlp_units, approximate=True).astype(jnp.bfloat16)
    out_source, in_weight = lax.optimization_barrier(
        (jnp.concatenate([attn_weight, down_weight], axis=0), in_weight)
    )
    out_weight = lax.all_gather(out_source, "seq", axis=1, tiled=True)
    terms_by_feature = lax.dot_general(
        out_weight,
        jnp.concatenate([attended, activated], axis=1),
        (((0,), (1,)), ((), ())),
        preferred_element_type=jnp.float32,
    )
    branch = lax.psum_scatter(
        terms_by_feature.astype(jnp.bfloat16), "wblk", scatter_dimension=0, tiled=True
    )
    branch = branch.T.reshape(prompts, local_len, dim_local).astype(jnp.float32)
    layer_out = hidden + modulation[2] * branch
    text_out = layer_out[:, :text_rows].astype(jnp.bfloat16)[None]
    image_out = layer_out[:, text_rows:]
    paired = lax.all_to_all(
        image_out[:, None].astype(jnp.bfloat16), "cfg", split_axis=0, concat_axis=1, tiled=True
    ).astype(jnp.float32)
    velocity = paired[:, 1] + guidance * (paired[:, 0] - paired[:, 1])
    own_prompts = prompts // 2
    latent = lax.dynamic_slice_in_dim(image_tokens, cfg_pos * own_prompts, own_prompts, 0).astype(
        jnp.float32
    )
    new_image = latent + step_size * velocity
    return (text_out, velocity, new_image)


def solution(mesh):
    in_specs = (
        P("cfg", None, "seq", "wblk"),
        P(None, "seq", "wblk"),
        P("cfg", "seq"),
        P("seq", None, "wblk"),
        P("seq", None, "wblk", None),
        P("seq", "wblk"),
        P(),
        P(),
        P("wblk", "seq"),
        P("wblk", "seq"),
        P(),
        P(),
    )
    out_specs = (P("cfg", None, "seq", "wblk"), P("cfg", "seq", "wblk"), P("cfg", "seq", "wblk"))
    return jax.shard_map(shards, mesh=mesh, in_specs=in_specs, out_specs=out_specs, check_vma=False)
```

```python
import math

import jax
import jax.numpy as jnp
from jax import lax
from jax.sharding import PartitionSpec as P

D = 3072
HD = 128
GRID = 64
STEPS = 28


epsilon = 1e-06
guidance = 3.5
time_shift = 3.0
rope_theta = 10000.0


def plan(timestep):
    step_index = timestep[0].astype(jnp.float32)
    time_now = 1.0 - step_index / STEPS
    time_next = 1.0 - (step_index + 1.0) / STEPS
    sigma_now = time_shift * time_now / (1.0 + (time_shift - 1.0) * time_now)
    sigma_next = time_shift * time_next / (1.0 + (time_shift - 1.0) * time_next)
    return (sigma_now, sigma_next - sigma_now)


def time_embedding(sigma_now, dim_count):
    halfwidth = dim_count // 2
    frequency = jnp.exp(-math.log(10000.0) * jnp.arange(halfwidth, dtype=jnp.float32) / halfwidth)
    angles = 1000.0 * sigma_now * frequency
    return jnp.concatenate([jnp.cos(angles), jnp.sin(angles)])


def inverse_freq(dim_count):
    return rope_theta ** (-jnp.arange(0, dim_count, 2, dtype=jnp.float32) / dim_count)


def rotary_angles(height_pos, width_pos):
    still_dims = HD // 8
    axis_dims = (HD - still_dims) // 2
    return jnp.concatenate(
        [
            jnp.zeros((height_pos.shape[0], still_dims // 2), jnp.float32),
            height_pos[:, None] * inverse_freq(axis_dims)[None],
            width_pos[:, None] * inverse_freq(axis_dims)[None],
        ],
        axis=1,
    )


def rotate(vectors, angles):
    paired_dims = vectors.reshape(vectors.shape[:-1] + (HD // 2, 2))
    cosine_table = jnp.cos(angles)[:, None, :]
    sine_table = jnp.sin(angles)[:, None, :]
    first_part = paired_dims[..., 0]
    second_part = paired_dims[..., 1]
    turned = jnp.stack(
        [
            first_part * cosine_table - second_part * sine_table,
            first_part * sine_table + second_part * cosine_table,
        ],
        axis=-1,
    )
    return turned.reshape(vectors.shape)


def head_norm(vectors, gain_vector):
    return (
        vectors
        * lax.rsqrt(jnp.mean(vectors * vectors, axis=-1, keepdims=True) + epsilon)
        * gain_vector
    )


def input_folder(source, pieces):
    width_rows = pieces[0].shape[0]
    first_total = jnp.dot(
        source, pieces[0].reshape(width_rows, -1), preferred_element_type=jnp.float32
    )
    second_total = jnp.dot(source, pieces[1], preferred_element_type=jnp.float32)
    return (first_total, second_total)


def output_folder(attended, activated, pieces):
    block_cols = jnp.dot(attended, pieces[0], preferred_element_type=jnp.float32)
    block_cols = block_cols + jnp.dot(activated, pieces[1], preferred_element_type=jnp.float32)
    return block_cols


def shards(
    text_tokens,
    image_tokens,
    pooled_vector,
    mod_weight,
    qkv_weight,
    up_weight,
    query_gain,
    key_gain,
    attn_weight,
    down_weight,
    lengths,
    timestep,
):
    seq_pos = lax.axis_index("seq")
    cfg_pos = lax.axis_index("cfg")
    prompts = image_tokens.shape[0]
    image_rows = image_tokens.shape[1]
    text_rows = text_tokens.shape[2]
    local_len = text_rows + image_rows
    dim_local = image_tokens.shape[2]
    dim_seq = pooled_vector.shape[1]
    heads_local = qkv_weight.shape[2]
    row_count = prompts * local_len
    sigma_now, step_size = plan(timestep)
    embedded = lax.dynamic_slice_in_dim(time_embedding(sigma_now, D), seq_pos * dim_seq, dim_seq)
    cond_vec = jax.nn.silu(pooled_vector[0] + embedded).astype(jnp.bfloat16)[None]
    mod_terms = jnp.dot(
        cond_vec, mod_weight.reshape(dim_seq, 3 * dim_local), preferred_element_type=jnp.float32
    )
    seq_count = lax.psum(1, "seq")
    mod_spread = jnp.broadcast_to(mod_terms.reshape(1, 3, dim_local), (seq_count, 3, dim_local))
    modulation = jnp.sum(lax.all_to_all(mod_spread, "seq", 0, 0, tiled=True), axis=0)
    local_rows = jnp.concatenate([text_tokens[0], image_tokens], axis=1)
    hidden = local_rows.astype(jnp.float32)
    totals, squares = lax.psum(
        (jnp.sum(hidden, axis=-1), jnp.sum(hidden * hidden, axis=-1)), "wblk"
    )
    average = (totals / D)[..., None]
    variance = (squares / D)[..., None] - average * average
    normed = (
        (hidden - average) * lax.rsqrt(variance + epsilon) * (1.0 + modulation[1]) + modulation[0]
    ).astype(jnp.bfloat16)
    width_rows = qkv_weight.shape[0]
    qkv_cols = 3 * heads_local * HD
    qkv_full = lax.all_gather(
        qkv_weight.reshape(width_rows, qkv_cols), "seq", axis=0, tiled=True
    )
    wblk_count = lax.psum(1, "wblk")
    spread = jnp.broadcast_to(normed.reshape(1, row_count, dim_local), (wblk_count, row_count, dim_local))
    gathered = lax.all_to_all(spread, "wblk", 0, 0, tiled=True)
    up_source, gathered = lax.optimization_barrier((up_weight, gathered))
    up_full = lax.all_gather(up_source, "seq", axis=0, tiled=True)
    projected = jnp.einsum(
        "wrf,wfn->rn",
        gathered,
        qkv_full.reshape(wblk_count, dim_local, -1),
        preferred_element_type=jnp.float32,
    )
    mlp_units = jnp.einsum(
        "wrf,wfn->rn",
        gathered,
        up_full.reshape(wblk_count, dim_local, -1),
        preferred_element_type=jnp.float32,
    )
    projected = projected.reshape(prompts, local_len, 3, heads_local, HD)
    image_index = seq_pos * image_rows + jnp.arange(image_rows, dtype=jnp.int32)
    height_pos = jnp.concatenate(
        [jnp.zeros((text_rows,), jnp.float32), (image_index // GRID).astype(jnp.float32)]
    )
    width_pos = jnp.concatenate(
        [jnp.zeros((text_rows,), jnp.float32), (image_index % GRID).astype(jnp.float32)]
    )
    angles = rotary_angles(height_pos, width_pos)
    queries = rotate(head_norm(projected[:, :, 0], query_gain), angles).astype(jnp.bfloat16)
    key_rows = rotate(head_norm(projected[:, :, 1], key_gain), angles).astype(jnp.bfloat16)
    values = projected[:, :, 2].astype(jnp.bfloat16)
    scale_factor = HD ** (-0.5)
    pair_count = prompts * heads_local
    subs = seq_count // pair_count
    sub_rows = local_len // subs
    pair_keys = key_rows.transpose(0, 2, 1, 3).reshape(pair_count, local_len, HD)
    pair_values = values.transpose(0, 2, 1, 3).reshape(pair_count, local_len, HD)
    pair_queries = queries.transpose(0, 2, 1, 3).reshape(seq_count, sub_rows, HD)
    send = jnp.concatenate(
        [
            jnp.broadcast_to(pair_keys[:, None], (pair_count, subs, local_len, HD)).reshape(
                seq_count, local_len, HD
            ),
            jnp.broadcast_to(pair_values[:, None], (pair_count, subs, local_len, HD)).reshape(
                seq_count, local_len, HD
            ),
            pair_queries,
        ],
        axis=1,
    )
    out_source, send = lax.optimization_barrier(
        (jnp.concatenate([attn_weight, down_weight], axis=0), send)
    )
    received = lax.all_to_all(send, "seq", 0, 0, tiled=True)
    key_piece = received[:, :local_len].reshape(seq_count * local_len, HD)
    value_piece = received[:, local_len : 2 * local_len].reshape(seq_count * local_len, HD)
    query_piece = received[:, 2 * local_len :].reshape(seq_count * sub_rows, HD)
    my_prompt = seq_pos // subs // heads_local
    width_keys = key_piece.shape[0]
    where_global = jnp.arange(width_keys, dtype=jnp.int32)
    shard_index = where_global // local_len
    within = where_global % local_len
    text_index = shard_index * text_rows + within
    key_live = (within >= text_rows) | (text_index < lengths[my_prompt])
    scores = (
        jnp.dot(query_piece, key_piece.T, preferred_element_type=jnp.float32) * scale_factor
    )
    scores = jnp.where(key_live[None, :], scores, -1e30)
    top_score = jnp.max(scores, axis=-1, keepdims=True)
    weights = jnp.exp(scores - top_score)
    denominator = jnp.sum(weights, axis=-1, keepdims=True)
    numerator = jnp.dot(
        weights.astype(jnp.bfloat16), value_piece, preferred_element_type=jnp.float32
    )
    mixed = (numerator / denominator).astype(jnp.bfloat16).reshape(seq_count, sub_rows, HD)
    returned = lax.all_to_all(mixed, "seq", 0, 0, tiled=True)
    attended = returned.reshape(prompts, heads_local, local_len, HD)
    attended = attended.transpose(0, 2, 1, 3).reshape(row_count, heads_local * HD)
    activated = jax.nn.gelu(mlp_units, approximate=True).astype(jnp.bfloat16)
    out_weight = lax.all_gather(out_source, "seq", axis=1, tiled=True)
    terms_by_feature = lax.dot_general(
        out_weight,
        jnp.concatenate([attended, activated], axis=1),
        (((0,), (1,)), ((), ())),
        preferred_element_type=jnp.float32,
    )
    branch = lax.psum_scatter(
        terms_by_feature.astype(jnp.bfloat16), "wblk", scatter_dimension=0, tiled=True
    )
    branch = branch.T.reshape(prompts, local_len, dim_local).astype(jnp.float32)
    layer_out = hidden + modulation[2] * branch
    text_out = layer_out[:, :text_rows].astype(jnp.bfloat16)[None]
    image_out = layer_out[:, text_rows:]
    paired = lax.all_to_all(
        image_out[:, None].astype(jnp.bfloat16), "cfg", split_axis=0, concat_axis=1, tiled=True
    ).astype(jnp.float32)
    velocity = paired[:, 1] + guidance * (paired[:, 0] - paired[:, 1])
    own_prompts = prompts // 2
    latent = lax.dynamic_slice_in_dim(image_tokens, cfg_pos * own_prompts, own_prompts, 0).astype(
        jnp.float32
    )
    new_image = latent + step_size * velocity
    return (text_out, velocity, new_image)


def solution(mesh):
    in_specs = (
        P("cfg", None, "seq", "wblk"),
        P(None, "seq", "wblk"),
        P("cfg", "seq"),
        P("seq", None, "wblk"),
        P("seq", None, "wblk", None),
        P("seq", "wblk"),
        P(),
        P(),
        P("wblk", "seq"),
        P("wblk", "seq"),
        P(),
        P(),
    )
    out_specs = (P("cfg", None, "seq", "wblk"), P("cfg", "seq", "wblk"), P("cfg", "seq", "wblk"))
    return jax.shard_map(shards, mesh=mesh, in_specs=in_specs, out_specs=out_specs, check_vma=False)
```

```python
import math

import jax
import jax.numpy as jnp
from jax import lax
from jax.sharding import PartitionSpec as P

D = 3072
HD = 128
GRID = 64
STEPS = 28


epsilon = 1e-06
guidance = 3.5
time_shift = 3.0
rope_theta = 10000.0


def plan(timestep):
    step_index = timestep[0].astype(jnp.float32)
    time_now = 1.0 - step_index / STEPS
    time_next = 1.0 - (step_index + 1.0) / STEPS
    sigma_now = time_shift * time_now / (1.0 + (time_shift - 1.0) * time_now)
    sigma_next = time_shift * time_next / (1.0 + (time_shift - 1.0) * time_next)
    return (sigma_now, sigma_next - sigma_now)


def time_embedding(sigma_now, dim_count):
    halfwidth = dim_count // 2
    frequency = jnp.exp(-math.log(10000.0) * jnp.arange(halfwidth, dtype=jnp.float32) / halfwidth)
    angles = 1000.0 * sigma_now * frequency
    return jnp.concatenate([jnp.cos(angles), jnp.sin(angles)])


def inverse_freq(dim_count):
    return rope_theta ** (-jnp.arange(0, dim_count, 2, dtype=jnp.float32) / dim_count)


def rotary_angles(height_pos, width_pos):
    still_dims = HD // 8
    axis_dims = (HD - still_dims) // 2
    return jnp.concatenate(
        [
            jnp.zeros((height_pos.shape[0], still_dims // 2), jnp.float32),
            height_pos[:, None] * inverse_freq(axis_dims)[None],
            width_pos[:, None] * inverse_freq(axis_dims)[None],
        ],
        axis=1,
    )


def rotate(vectors, angles):
    paired_dims = vectors.reshape(vectors.shape[:-1] + (HD // 2, 2))
    cosine_table = jnp.cos(angles)[:, None, :]
    sine_table = jnp.sin(angles)[:, None, :]
    first_part = paired_dims[..., 0]
    second_part = paired_dims[..., 1]
    turned = jnp.stack(
        [
            first_part * cosine_table - second_part * sine_table,
            first_part * sine_table + second_part * cosine_table,
        ],
        axis=-1,
    )
    return turned.reshape(vectors.shape)


def head_norm(vectors, gain_vector):
    return (
        vectors
        * lax.rsqrt(jnp.mean(vectors * vectors, axis=-1, keepdims=True) + epsilon)
        * gain_vector
    )


def input_folder(source, pieces):
    width_rows = pieces[0].shape[0]
    first_total = jnp.dot(
        source, pieces[0].reshape(width_rows, -1), preferred_element_type=jnp.float32
    )
    second_total = jnp.dot(source, pieces[1], preferred_element_type=jnp.float32)
    return (first_total, second_total)


def output_folder(attended, activated, pieces):
    block_cols = jnp.dot(attended, pieces[0], preferred_element_type=jnp.float32)
    block_cols = block_cols + jnp.dot(activated, pieces[1], preferred_element_type=jnp.float32)
    return block_cols


def shards(
    text_tokens,
    image_tokens,
    pooled_vector,
    mod_weight,
    qkv_weight,
    up_weight,
    query_gain,
    key_gain,
    attn_weight,
    down_weight,
    lengths,
    timestep,
):
    seq_pos = lax.axis_index("seq")
    cfg_pos = lax.axis_index("cfg")
    prompts = image_tokens.shape[0]
    image_rows = image_tokens.shape[1]
    text_rows = text_tokens.shape[2]
    local_len = text_rows + image_rows
    dim_local = image_tokens.shape[2]
    dim_seq = pooled_vector.shape[1]
    heads_local = qkv_weight.shape[2]
    row_count = prompts * local_len
    sigma_now, step_size = plan(timestep)
    embedded = lax.dynamic_slice_in_dim(time_embedding(sigma_now, D), seq_pos * dim_seq, dim_seq)
    cond_vec = jax.nn.silu(pooled_vector[0] + embedded).astype(jnp.bfloat16)[None]
    mod_terms = jnp.dot(
        cond_vec, mod_weight.reshape(dim_seq, 3 * dim_local), preferred_element_type=jnp.float32
    )
    seq_count = lax.psum(1, "seq")
    mod_spread = jnp.broadcast_to(mod_terms.reshape(1, 3, dim_local), (seq_count, 3, dim_local))
    modulation = jnp.sum(lax.all_to_all(mod_spread, "seq", 0, 0, tiled=True), axis=0)
    local_rows = jnp.concatenate([text_tokens[0], image_tokens], axis=1)
    hidden = local_rows.astype(jnp.float32)
    totals, squares = lax.psum(
        (jnp.sum(hidden, axis=-1), jnp.sum(hidden * hidden, axis=-1)), "wblk"
    )
    average = (totals / D)[..., None]
    variance = (squares / D)[..., None] - average * average
    normed = (
        (hidden - average) * lax.rsqrt(variance + epsilon) * (1.0 + modulation[1]) + modulation[0]
    ).astype(jnp.bfloat16)
    width_rows = qkv_weight.shape[0]
    qkv_cols = 3 * heads_local * HD
    qkv_full = lax.all_gather(
        qkv_weight.reshape(width_rows, qkv_cols), "seq", axis=0, tiled=True
    )
    wblk_count = lax.psum(1, "wblk")
    spread = jnp.broadcast_to(normed.reshape(1, row_count, dim_local), (wblk_count, row_count, dim_local))
    gathered = lax.all_to_all(spread, "wblk", 0, 0, tiled=True)
    up_cols = up_weight.shape[1]
    tail_source = jnp.concatenate(
        [up_weight, jnp.concatenate([attn_weight, down_weight], axis=0).T], axis=1
    )
    tail_source, gathered = lax.optimization_barrier((tail_source, gathered))
    tail_full = lax.all_gather(tail_source, "seq", axis=0, tiled=True)
    up_full = tail_full[:, :up_cols]
    projected = jnp.einsum(
        "wrf,wfn->rn",
        gathered,
        qkv_full.reshape(wblk_count, dim_local, -1),
        preferred_element_type=jnp.float32,
    )
    mlp_units = jnp.einsum(
        "wrf,wfn->rn",
        gathered,
        up_full.reshape(wblk_count, dim_local, -1),
        preferred_element_type=jnp.float32,
    )
    projected = projected.reshape(prompts, local_len, 3, heads_local, HD)
    image_index = seq_pos * image_rows + jnp.arange(image_rows, dtype=jnp.int32)
    height_pos = jnp.concatenate(
        [jnp.zeros((text_rows,), jnp.float32), (image_index // GRID).astype(jnp.float32)]
    )
    width_pos = jnp.concatenate(
        [jnp.zeros((text_rows,), jnp.float32), (image_index % GRID).astype(jnp.float32)]
    )
    angles = rotary_angles(height_pos, width_pos)
    queries = rotate(head_norm(projected[:, :, 0], query_gain), angles).astype(jnp.bfloat16)
    key_rows = rotate(head_norm(projected[:, :, 1], key_gain), angles).astype(jnp.bfloat16)
    values = projected[:, :, 2].astype(jnp.bfloat16)
    scale_factor = HD ** (-0.5)
    pair_count = prompts * heads_local
    subs = seq_count // pair_count
    sub_rows = local_len // subs
    pair_keys = key_rows.transpose(0, 2, 1, 3).reshape(pair_count, local_len, HD)
    pair_values = values.transpose(0, 2, 1, 3).reshape(pair_count, local_len, HD)
    pair_queries = queries.transpose(0, 2, 1, 3).reshape(seq_count, sub_rows, HD)
    send = jnp.concatenate(
        [
            jnp.broadcast_to(pair_keys[:, None], (pair_count, subs, local_len, HD)).reshape(
                seq_count, local_len, HD
            ),
            jnp.broadcast_to(pair_values[:, None], (pair_count, subs, local_len, HD)).reshape(
                seq_count, local_len, HD
            ),
            pair_queries,
        ],
        axis=1,
    )
    received = lax.all_to_all(send, "seq", 0, 0, tiled=True)
    key_piece = received[:, :local_len].reshape(seq_count * local_len, HD)
    value_piece = received[:, local_len : 2 * local_len].reshape(seq_count * local_len, HD)
    query_piece = received[:, 2 * local_len :].reshape(seq_count * sub_rows, HD)
    my_prompt = seq_pos // subs // heads_local
    width_keys = key_piece.shape[0]
    where_global = jnp.arange(width_keys, dtype=jnp.int32)
    shard_index = where_global // local_len
    within = where_global % local_len
    text_index = shard_index * text_rows + within
    key_live = (within >= text_rows) | (text_index < lengths[my_prompt])
    scores = (
        jnp.dot(query_piece, key_piece.T, preferred_element_type=jnp.float32) * scale_factor
    )
    scores = jnp.where(key_live[None, :], scores, -1e30)
    top_score = jnp.max(scores, axis=-1, keepdims=True)
    weights = jnp.exp(scores - top_score)
    denominator = jnp.sum(weights, axis=-1, keepdims=True)
    numerator = jnp.dot(
        weights.astype(jnp.bfloat16), value_piece, preferred_element_type=jnp.float32
    )
    mixed = (numerator / denominator).astype(jnp.bfloat16).reshape(seq_count, sub_rows, HD)
    returned = lax.all_to_all(mixed, "seq", 0, 0, tiled=True)
    attended = returned.reshape(prompts, heads_local, local_len, HD)
    attended = attended.transpose(0, 2, 1, 3).reshape(row_count, heads_local * HD)
    activated = jax.nn.gelu(mlp_units, approximate=True).astype(jnp.bfloat16)
    terms_by_feature = lax.dot_general(
        tail_full[:, up_cols:],
        jnp.concatenate([attended, activated], axis=1),
        (((1,), (1,)), ((), ())),
        preferred_element_type=jnp.float32,
    )
    branch = lax.psum_scatter(
        terms_by_feature.astype(jnp.bfloat16), "wblk", scatter_dimension=0, tiled=True
    )
    branch = branch.T.reshape(prompts, local_len, dim_local).astype(jnp.float32)
    layer_out = hidden + modulation[2] * branch
    text_out = layer_out[:, :text_rows].astype(jnp.bfloat16)[None]
    image_out = layer_out[:, text_rows:]
    paired = lax.all_to_all(
        image_out[:, None].astype(jnp.bfloat16), "cfg", split_axis=0, concat_axis=1, tiled=True
    ).astype(jnp.float32)
    velocity = paired[:, 1] + guidance * (paired[:, 0] - paired[:, 1])
    own_prompts = prompts // 2
    latent = lax.dynamic_slice_in_dim(image_tokens, cfg_pos * own_prompts, own_prompts, 0).astype(
        jnp.float32
    )
    new_image = latent + step_size * velocity
    return (text_out, velocity, new_image)


def solution(mesh):
    in_specs = (
        P("cfg", None, "seq", "wblk"),
        P(None, "seq", "wblk"),
        P("cfg", "seq"),
        P("seq", None, "wblk"),
        P("seq", None, "wblk", None),
        P("seq", "wblk"),
        P(),
        P(),
        P("wblk", "seq"),
        P("wblk", "seq"),
        P(),
        P(),
    )
    out_specs = (P("cfg", None, "seq", "wblk"), P("cfg", "seq", "wblk"), P("cfg", "seq", "wblk"))
    return jax.shard_map(shards, mesh=mesh, in_specs=in_specs, out_specs=out_specs, check_vma=False)
```

```python
import math

import jax
import jax.numpy as jnp
from jax import lax
from jax.sharding import PartitionSpec as P

D = 3072
HD = 128
GRID = 64
STEPS = 28


epsilon = 1e-06
guidance = 3.5
time_shift = 3.0
rope_theta = 10000.0


def plan(timestep):
    step_index = timestep[0].astype(jnp.float32)
    time_now = 1.0 - step_index / STEPS
    time_next = 1.0 - (step_index + 1.0) / STEPS
    sigma_now = time_shift * time_now / (1.0 + (time_shift - 1.0) * time_now)
    sigma_next = time_shift * time_next / (1.0 + (time_shift - 1.0) * time_next)
    return (sigma_now, sigma_next - sigma_now)


def time_embedding(sigma_now, dim_count):
    halfwidth = dim_count // 2
    frequency = jnp.exp(-math.log(10000.0) * jnp.arange(halfwidth, dtype=jnp.float32) / halfwidth)
    angles = 1000.0 * sigma_now * frequency
    return jnp.concatenate([jnp.cos(angles), jnp.sin(angles)])


def inverse_freq(dim_count):
    return rope_theta ** (-jnp.arange(0, dim_count, 2, dtype=jnp.float32) / dim_count)


def rotary_angles(height_pos, width_pos):
    still_dims = HD // 8
    axis_dims = (HD - still_dims) // 2
    return jnp.concatenate(
        [
            jnp.zeros((height_pos.shape[0], still_dims // 2), jnp.float32),
            height_pos[:, None] * inverse_freq(axis_dims)[None],
            width_pos[:, None] * inverse_freq(axis_dims)[None],
        ],
        axis=1,
    )


def rotate(vectors, angles):
    paired_dims = vectors.reshape(vectors.shape[:-1] + (HD // 2, 2))
    cosine_table = jnp.cos(angles)[:, None, :]
    sine_table = jnp.sin(angles)[:, None, :]
    first_part = paired_dims[..., 0]
    second_part = paired_dims[..., 1]
    turned = jnp.stack(
        [
            first_part * cosine_table - second_part * sine_table,
            first_part * sine_table + second_part * cosine_table,
        ],
        axis=-1,
    )
    return turned.reshape(vectors.shape)


def head_norm(vectors, gain_vector):
    return (
        vectors
        * lax.rsqrt(jnp.mean(vectors * vectors, axis=-1, keepdims=True) + epsilon)
        * gain_vector
    )


def input_folder(source, pieces):
    width_rows = pieces[0].shape[0]
    first_total = jnp.dot(
        source, pieces[0].reshape(width_rows, -1), preferred_element_type=jnp.float32
    )
    second_total = jnp.dot(source, pieces[1], preferred_element_type=jnp.float32)
    return (first_total, second_total)


def output_folder(attended, activated, pieces):
    block_cols = jnp.dot(attended, pieces[0], preferred_element_type=jnp.float32)
    block_cols = block_cols + jnp.dot(activated, pieces[1], preferred_element_type=jnp.float32)
    return block_cols


def shards(
    text_tokens,
    image_tokens,
    pooled_vector,
    mod_weight,
    qkv_weight,
    up_weight,
    query_gain,
    key_gain,
    attn_weight,
    down_weight,
    lengths,
    timestep,
):
    seq_pos = lax.axis_index("seq")
    cfg_pos = lax.axis_index("cfg")
    prompts = image_tokens.shape[0]
    image_rows = image_tokens.shape[1]
    text_rows = text_tokens.shape[2]
    local_len = text_rows + image_rows
    dim_local = image_tokens.shape[2]
    dim_seq = pooled_vector.shape[1]
    heads_local = qkv_weight.shape[2]
    row_count = prompts * local_len
    sigma_now, step_size = plan(timestep)
    embedded = lax.dynamic_slice_in_dim(time_embedding(sigma_now, D), seq_pos * dim_seq, dim_seq)
    cond_vec = jax.nn.silu(pooled_vector[0] + embedded).astype(jnp.bfloat16)[None]
    mod_terms = jnp.dot(
        cond_vec, mod_weight.reshape(dim_seq, 3 * dim_local), preferred_element_type=jnp.float32
    )
    seq_count = lax.psum(1, "seq")
    mod_spread = jnp.broadcast_to(mod_terms.reshape(1, 3, dim_local), (seq_count, 3, dim_local))
    modulation = jnp.sum(lax.all_to_all(mod_spread, "seq", 0, 0, tiled=True), axis=0)
    local_rows = jnp.concatenate([text_tokens[0], image_tokens], axis=1)
    hidden = local_rows.astype(jnp.float32)
    totals, squares = lax.psum(
        (jnp.sum(hidden, axis=-1), jnp.sum(hidden * hidden, axis=-1)), "wblk"
    )
    average = (totals / D)[..., None]
    variance = (squares / D)[..., None] - average * average
    normed = (
        (hidden - average) * lax.rsqrt(variance + epsilon) * (1.0 + modulation[1]) + modulation[0]
    ).astype(jnp.bfloat16)
    width_rows = qkv_weight.shape[0]
    qkv_cols = 3 * heads_local * HD
    qkv_full = lax.all_gather(
        qkv_weight.reshape(width_rows, qkv_cols), "seq", axis=0, tiled=True
    )
    wblk_count = lax.psum(1, "wblk")
    spread = jnp.broadcast_to(normed.reshape(1, row_count, dim_local), (wblk_count, row_count, dim_local))
    gathered = lax.all_to_all(spread, "wblk", 0, 0, tiled=True)
    up_cols = up_weight.shape[1]
    tail_source = jnp.concatenate(
        [up_weight, jnp.concatenate([attn_weight, down_weight], axis=0).T], axis=1
    )
    tail_source, gathered = lax.optimization_barrier((tail_source, gathered))
    tail_full = lax.all_gather(tail_source, "seq", axis=0, tiled=True)
    up_full = tail_full[:, :up_cols]
    projected = jnp.einsum(
        "wrf,wfn->rn",
        gathered,
        qkv_full.reshape(wblk_count, dim_local, -1),
        preferred_element_type=jnp.float32,
    )
    mlp_units = jnp.einsum(
        "wrf,wfn->rn",
        gathered,
        up_full.reshape(wblk_count, dim_local, -1),
        preferred_element_type=jnp.float32,
    )
    projected = projected.reshape(prompts, local_len, 3, heads_local, HD)
    image_index = seq_pos * image_rows + jnp.arange(image_rows, dtype=jnp.int32)
    height_pos = jnp.concatenate(
        [jnp.zeros((text_rows,), jnp.float32), (image_index // GRID).astype(jnp.float32)]
    )
    width_pos = jnp.concatenate(
        [jnp.zeros((text_rows,), jnp.float32), (image_index % GRID).astype(jnp.float32)]
    )
    angles = rotary_angles(height_pos, width_pos)
    queries = rotate(head_norm(projected[:, :, 0], query_gain), angles).astype(jnp.bfloat16)
    key_rows = rotate(head_norm(projected[:, :, 1], key_gain), angles).astype(jnp.bfloat16)
    values = projected[:, :, 2].astype(jnp.bfloat16)
    scale_factor = HD ** (-0.5)
    pair_count = prompts * heads_local
    subs = seq_count // pair_count
    sub_rows = local_len // subs
    pair_keys = key_rows.transpose(0, 2, 1, 3).reshape(pair_count, local_len, HD)
    pair_values = values.transpose(0, 2, 1, 3).reshape(pair_count, local_len, HD)
    pair_queries = queries.transpose(0, 2, 1, 3).reshape(seq_count, sub_rows, HD)
    send = jnp.concatenate(
        [
            jnp.broadcast_to(pair_keys[:, None], (pair_count, subs, local_len, HD)).reshape(
                seq_count, local_len, HD
            ),
            jnp.broadcast_to(pair_values[:, None], (pair_count, subs, local_len, HD)).reshape(
                seq_count, local_len, HD
            ),
            pair_queries,
        ],
        axis=1,
    )
    received = lax.all_to_all(send, "seq", 0, 0, tiled=True)
    key_piece = received[:, :local_len].reshape(seq_count * local_len, HD)
    value_piece = received[:, local_len : 2 * local_len].reshape(seq_count * local_len, HD)
    query_piece = received[:, 2 * local_len :].reshape(seq_count * sub_rows, HD)
    my_prompt = seq_pos // subs // heads_local
    width_keys = key_piece.shape[0]
    where_global = jnp.arange(width_keys, dtype=jnp.int32)
    shard_index = where_global // local_len
    within = where_global % local_len
    text_index = shard_index * text_rows + within
    key_live = (within >= text_rows) | (text_index < lengths[my_prompt])
    scores = (
        jnp.dot(query_piece, key_piece.T, preferred_element_type=jnp.float32) * scale_factor
    )
    scores = jnp.where(key_live[None, :], scores, -1e30)
    top_score = jnp.max(scores, axis=-1, keepdims=True)
    weights = jnp.exp(scores - top_score)
    denominator = jnp.sum(weights, axis=-1, keepdims=True)
    numerator = jnp.dot(
        weights.astype(jnp.bfloat16), value_piece, preferred_element_type=jnp.float32
    )
    mixed = (numerator / denominator).astype(jnp.bfloat16).reshape(seq_count, sub_rows, HD)
    returned = lax.all_to_all(mixed, "seq", 0, 0, tiled=True)
    attended = returned.reshape(prompts, heads_local, local_len, HD)
    attended = attended.transpose(0, 2, 1, 3).reshape(row_count, heads_local * HD)
    activated = jax.nn.gelu(mlp_units, approximate=True).astype(jnp.bfloat16)
    out_weight_t = tail_full[:, up_cols:]
    mixed_rows = jnp.concatenate([attended, activated], axis=1)
    first_rows = mixed_rows[:local_len]
    second_rows = mixed_rows[local_len:]
    first_terms = lax.dot_general(
        out_weight_t, first_rows, (((1,), (1,)), ((), ())), preferred_element_type=jnp.float32
    )
    second_terms = lax.dot_general(
        out_weight_t, second_rows, (((1,), (1,)), ((), ())), preferred_element_type=jnp.float32
    )
    first_branch = lax.psum_scatter(
        first_terms.astype(jnp.bfloat16), "wblk", scatter_dimension=0, tiled=True
    ).astype(jnp.float32)
    second_parts = lax.all_to_all(
        second_terms.astype(jnp.bfloat16).reshape(wblk_count, dim_local, -1), "wblk", 0, 0, tiled=True
    )
    second_branch = jnp.sum(second_parts.astype(jnp.float32), axis=0)
    branch = jnp.stack([first_branch.T, second_branch.T])
    layer_out = hidden + modulation[2] * branch
    text_out = layer_out[:, :text_rows].astype(jnp.bfloat16)[None]
    image_out = layer_out[:, text_rows:]
    paired = lax.all_to_all(
        image_out[:, None].astype(jnp.bfloat16), "cfg", split_axis=0, concat_axis=1, tiled=True
    ).astype(jnp.float32)
    velocity = paired[:, 1] + guidance * (paired[:, 0] - paired[:, 1])
    own_prompts = prompts // 2
    latent = lax.dynamic_slice_in_dim(image_tokens, cfg_pos * own_prompts, own_prompts, 0).astype(
        jnp.float32
    )
    new_image = latent + step_size * velocity
    return (text_out, velocity, new_image)


def solution(mesh):
    in_specs = (
        P("cfg", None, "seq", "wblk"),
        P(None, "seq", "wblk"),
        P("cfg", "seq"),
        P("seq", None, "wblk"),
        P("seq", None, "wblk", None),
        P("seq", "wblk"),
        P(),
        P(),
        P("wblk", "seq"),
        P("wblk", "seq"),
        P(),
        P(),
    )
    out_specs = (P("cfg", None, "seq", "wblk"), P("cfg", "seq", "wblk"), P("cfg", "seq", "wblk"))
    return jax.shard_map(shards, mesh=mesh, in_specs=in_specs, out_specs=out_specs, check_vma=False)
```

```python
import math

import jax
import jax.numpy as jnp
from jax import lax
from jax.sharding import PartitionSpec as P

D = 3072
HD = 128
GRID = 64
STEPS = 28


epsilon = 1e-06
guidance = 3.5
time_shift = 3.0
rope_theta = 10000.0


def plan(timestep):
    step_index = timestep[0].astype(jnp.float32)
    time_now = 1.0 - step_index / STEPS
    time_next = 1.0 - (step_index + 1.0) / STEPS
    sigma_now = time_shift * time_now / (1.0 + (time_shift - 1.0) * time_now)
    sigma_next = time_shift * time_next / (1.0 + (time_shift - 1.0) * time_next)
    return (sigma_now, sigma_next - sigma_now)


def time_embedding(sigma_now, dim_count):
    halfwidth = dim_count // 2
    frequency = jnp.exp(-math.log(10000.0) * jnp.arange(halfwidth, dtype=jnp.float32) / halfwidth)
    angles = 1000.0 * sigma_now * frequency
    return jnp.concatenate([jnp.cos(angles), jnp.sin(angles)])


def inverse_freq(dim_count):
    return rope_theta ** (-jnp.arange(0, dim_count, 2, dtype=jnp.float32) / dim_count)


def rotary_angles(height_pos, width_pos):
    still_dims = HD // 8
    axis_dims = (HD - still_dims) // 2
    return jnp.concatenate(
        [
            jnp.zeros((height_pos.shape[0], still_dims // 2), jnp.float32),
            height_pos[:, None] * inverse_freq(axis_dims)[None],
            width_pos[:, None] * inverse_freq(axis_dims)[None],
        ],
        axis=1,
    )


def rotate(vectors, angles):
    paired_dims = vectors.reshape(vectors.shape[:-1] + (HD // 2, 2))
    cosine_table = jnp.cos(angles)[:, None, :]
    sine_table = jnp.sin(angles)[:, None, :]
    first_part = paired_dims[..., 0]
    second_part = paired_dims[..., 1]
    turned = jnp.stack(
        [
            first_part * cosine_table - second_part * sine_table,
            first_part * sine_table + second_part * cosine_table,
        ],
        axis=-1,
    )
    return turned.reshape(vectors.shape)


def head_norm(vectors, gain_vector):
    return (
        vectors
        * lax.rsqrt(jnp.mean(vectors * vectors, axis=-1, keepdims=True) + epsilon)
        * gain_vector
    )


def input_folder(source, pieces):
    width_rows = pieces[0].shape[0]
    first_total = jnp.dot(
        source, pieces[0].reshape(width_rows, -1), preferred_element_type=jnp.float32
    )
    second_total = jnp.dot(source, pieces[1], preferred_element_type=jnp.float32)
    return (first_total, second_total)


def output_folder(attended, activated, pieces):
    block_cols = jnp.dot(attended, pieces[0], preferred_element_type=jnp.float32)
    block_cols = block_cols + jnp.dot(activated, pieces[1], preferred_element_type=jnp.float32)
    return block_cols


def shards(
    text_tokens,
    image_tokens,
    pooled_vector,
    mod_weight,
    qkv_weight,
    up_weight,
    query_gain,
    key_gain,
    attn_weight,
    down_weight,
    lengths,
    timestep,
):
    seq_pos = lax.axis_index("seq")
    cfg_pos = lax.axis_index("cfg")
    prompts = image_tokens.shape[0]
    image_rows = image_tokens.shape[1]
    text_rows = text_tokens.shape[2]
    local_len = text_rows + image_rows
    dim_local = image_tokens.shape[2]
    dim_seq = pooled_vector.shape[1]
    heads_local = qkv_weight.shape[2]
    row_count = prompts * local_len
    sigma_now, step_size = plan(timestep)
    embedded = lax.dynamic_slice_in_dim(time_embedding(sigma_now, D), seq_pos * dim_seq, dim_seq)
    cond_vec = jax.nn.silu(pooled_vector[0] + embedded).astype(jnp.bfloat16)[None]
    mod_terms = jnp.dot(
        cond_vec, mod_weight.reshape(dim_seq, 3 * dim_local), preferred_element_type=jnp.float32
    )
    seq_count = lax.psum(1, "seq")
    mod_spread = jnp.broadcast_to(mod_terms.reshape(1, 3, dim_local), (seq_count, 3, dim_local))
    modulation = jnp.sum(lax.all_to_all(mod_spread, "seq", 0, 0, tiled=True), axis=0)
    local_rows = jnp.concatenate([text_tokens[0], image_tokens], axis=1)
    hidden = local_rows.astype(jnp.float32)
    totals, squares = lax.psum(
        (jnp.sum(hidden, axis=-1), jnp.sum(hidden * hidden, axis=-1)), "wblk"
    )
    average = (totals / D)[..., None]
    variance = (squares / D)[..., None] - average * average
    normed = (
        (hidden - average) * lax.rsqrt(variance + epsilon) * (1.0 + modulation[1]) + modulation[0]
    ).astype(jnp.bfloat16)
    width_rows = qkv_weight.shape[0]
    qkv_cols = 3 * heads_local * HD
    qkv_full = lax.all_gather(
        qkv_weight.reshape(width_rows, qkv_cols), "seq", axis=0, tiled=True
    )
    wblk_count = lax.psum(1, "wblk")
    spread = jnp.broadcast_to(normed.reshape(1, row_count, dim_local), (wblk_count, row_count, dim_local))
    gathered = lax.all_to_all(spread, "wblk", 0, 0, tiled=True)
    up_cols = up_weight.shape[1]
    tail_source = jnp.concatenate(
        [up_weight, jnp.concatenate([attn_weight, down_weight], axis=0).T], axis=1
    )
    tail_source, gathered = lax.optimization_barrier((tail_source, gathered))
    tail_full = lax.all_gather(tail_source, "seq", axis=0, tiled=True)
    up_full = tail_full[:, :up_cols]
    projected = jnp.einsum(
        "wrf,wfn->rn",
        gathered,
        qkv_full.reshape(wblk_count, dim_local, -1),
        preferred_element_type=jnp.float32,
    )
    mlp_units = jnp.einsum(
        "wrf,wfn->rn",
        gathered,
        up_full.reshape(wblk_count, dim_local, -1),
        preferred_element_type=jnp.float32,
    )
    projected = projected.reshape(prompts, local_len, 3, heads_local, HD)
    image_index = seq_pos * image_rows + jnp.arange(image_rows, dtype=jnp.int32)
    height_pos = jnp.concatenate(
        [jnp.zeros((text_rows,), jnp.float32), (image_index // GRID).astype(jnp.float32)]
    )
    width_pos = jnp.concatenate(
        [jnp.zeros((text_rows,), jnp.float32), (image_index % GRID).astype(jnp.float32)]
    )
    angles = rotary_angles(height_pos, width_pos)
    queries = rotate(head_norm(projected[:, :, 0], query_gain), angles).astype(jnp.bfloat16)
    key_rows = rotate(head_norm(projected[:, :, 1], key_gain), angles).astype(jnp.bfloat16)
    values = projected[:, :, 2].astype(jnp.bfloat16)
    scale_factor = HD ** (-0.5)
    pair_count = prompts * heads_local
    subs = seq_count // pair_count
    sub_rows = local_len // subs
    pair_keys = key_rows.transpose(0, 2, 1, 3).reshape(pair_count, local_len, HD)
    pair_values = values.transpose(0, 2, 1, 3).reshape(pair_count, local_len, HD)
    pair_queries = queries.transpose(0, 2, 1, 3).reshape(seq_count, sub_rows, HD)
    send = jnp.concatenate(
        [
            jnp.broadcast_to(pair_keys[:, None], (pair_count, subs, local_len, HD)).reshape(
                seq_count, local_len, HD
            ),
            jnp.broadcast_to(pair_values[:, None], (pair_count, subs, local_len, HD)).reshape(
                seq_count, local_len, HD
            ),
            pair_queries,
        ],
        axis=1,
    )
    received = lax.all_to_all(send, "seq", 0, 0, tiled=True)
    key_piece = received[:, :local_len].reshape(seq_count * local_len, HD)
    value_piece = received[:, local_len : 2 * local_len].reshape(seq_count * local_len, HD)
    query_piece = received[:, 2 * local_len :].reshape(seq_count * sub_rows, HD)
    my_prompt = seq_pos // subs // heads_local
    width_keys = key_piece.shape[0]
    where_global = jnp.arange(width_keys, dtype=jnp.int32)
    shard_index = where_global // local_len
    within = where_global % local_len
    text_index = shard_index * text_rows + within
    key_live = (within >= text_rows) | (text_index < lengths[my_prompt])
    scores = (
        jnp.dot(query_piece, key_piece.T, preferred_element_type=jnp.float32) * scale_factor
    )
    scores = jnp.where(key_live[None, :], scores, -1e30)
    top_score = jnp.max(scores, axis=-1, keepdims=True)
    weights = jnp.exp(scores - top_score)
    denominator = jnp.sum(weights, axis=-1, keepdims=True)
    numerator = jnp.dot(
        weights.astype(jnp.bfloat16), value_piece, preferred_element_type=jnp.float32
    )
    mixed = (numerator / denominator).astype(jnp.bfloat16).reshape(seq_count, sub_rows, HD)
    returned = lax.all_to_all(mixed, "seq", 0, 0, tiled=True)
    attended = returned.reshape(prompts, heads_local, local_len, HD)
    attended = attended.transpose(0, 2, 1, 3).reshape(row_count, heads_local * HD)
    activated = jax.nn.gelu(mlp_units, approximate=True).astype(jnp.bfloat16)
    block_terms = jnp.einsum(
        "bjk,rk->brj",
        tail_full[:, up_cols:].reshape(wblk_count, dim_local, -1),
        jnp.concatenate([attended, activated], axis=1),
        preferred_element_type=jnp.float32,
    )
    branch = lax.psum_scatter(
        block_terms.astype(jnp.bfloat16), "wblk", scatter_dimension=0, tiled=True
    )
    branch = branch.reshape(prompts, local_len, dim_local).astype(jnp.float32)
    layer_out = hidden + modulation[2] * branch
    text_out = layer_out[:, :text_rows].astype(jnp.bfloat16)[None]
    image_out = layer_out[:, text_rows:]
    paired = lax.all_to_all(
        image_out[:, None].astype(jnp.bfloat16), "cfg", split_axis=0, concat_axis=1, tiled=True
    ).astype(jnp.float32)
    velocity = paired[:, 1] + guidance * (paired[:, 0] - paired[:, 1])
    own_prompts = prompts // 2
    latent = lax.dynamic_slice_in_dim(image_tokens, cfg_pos * own_prompts, own_prompts, 0).astype(
        jnp.float32
    )
    new_image = latent + step_size * velocity
    return (text_out, velocity, new_image)


def solution(mesh):
    in_specs = (
        P("cfg", None, "seq", "wblk"),
        P(None, "seq", "wblk"),
        P("cfg", "seq"),
        P("seq", None, "wblk"),
        P("seq", None, "wblk", None),
        P("seq", "wblk"),
        P(),
        P(),
        P("wblk", "seq"),
        P("wblk", "seq"),
        P(),
        P(),
    )
    out_specs = (P("cfg", None, "seq", "wblk"), P("cfg", "seq", "wblk"), P("cfg", "seq", "wblk"))
    return jax.shard_map(shards, mesh=mesh, in_specs=in_specs, out_specs=out_specs, check_vma=False)
```

```python
import math

import jax
import jax.numpy as jnp
from jax import lax
from jax.sharding import PartitionSpec as P

D = 3072
HD = 128
GRID = 64
STEPS = 28


epsilon = 1e-06
guidance = 3.5
time_shift = 3.0
rope_theta = 10000.0


def plan(timestep):
    step_index = timestep[0].astype(jnp.float32)
    time_now = 1.0 - step_index / STEPS
    time_next = 1.0 - (step_index + 1.0) / STEPS
    sigma_now = time_shift * time_now / (1.0 + (time_shift - 1.0) * time_now)
    sigma_next = time_shift * time_next / (1.0 + (time_shift - 1.0) * time_next)
    return (sigma_now, sigma_next - sigma_now)


def time_embedding(sigma_now, dim_count):
    halfwidth = dim_count // 2
    frequency = jnp.exp(-math.log(10000.0) * jnp.arange(halfwidth, dtype=jnp.float32) / halfwidth)
    angles = 1000.0 * sigma_now * frequency
    return jnp.concatenate([jnp.cos(angles), jnp.sin(angles)])


def inverse_freq(dim_count):
    return rope_theta ** (-jnp.arange(0, dim_count, 2, dtype=jnp.float32) / dim_count)


def rotary_angles(height_pos, width_pos):
    still_dims = HD // 8
    axis_dims = (HD - still_dims) // 2
    return jnp.concatenate(
        [
            jnp.zeros((height_pos.shape[0], still_dims // 2), jnp.float32),
            height_pos[:, None] * inverse_freq(axis_dims)[None],
            width_pos[:, None] * inverse_freq(axis_dims)[None],
        ],
        axis=1,
    )


def rotate(vectors, angles):
    paired_dims = vectors.reshape(vectors.shape[:-1] + (HD // 2, 2))
    cosine_table = jnp.cos(angles)[:, None, :]
    sine_table = jnp.sin(angles)[:, None, :]
    first_part = paired_dims[..., 0]
    second_part = paired_dims[..., 1]
    turned = jnp.stack(
        [
            first_part * cosine_table - second_part * sine_table,
            first_part * sine_table + second_part * cosine_table,
        ],
        axis=-1,
    )
    return turned.reshape(vectors.shape)


def head_norm(vectors, gain_vector):
    return (
        vectors
        * lax.rsqrt(jnp.mean(vectors * vectors, axis=-1, keepdims=True) + epsilon)
        * gain_vector
    )


def input_folder(source, pieces):
    width_rows = pieces[0].shape[0]
    first_total = jnp.dot(
        source, pieces[0].reshape(width_rows, -1), preferred_element_type=jnp.float32
    )
    second_total = jnp.dot(source, pieces[1], preferred_element_type=jnp.float32)
    return (first_total, second_total)


def output_folder(attended, activated, pieces):
    block_cols = jnp.dot(attended, pieces[0], preferred_element_type=jnp.float32)
    block_cols = block_cols + jnp.dot(activated, pieces[1], preferred_element_type=jnp.float32)
    return block_cols


def shards(
    text_tokens,
    image_tokens,
    pooled_vector,
    mod_weight,
    qkv_weight,
    up_weight,
    query_gain,
    key_gain,
    attn_weight,
    down_weight,
    lengths,
    timestep,
):
    seq_pos = lax.axis_index("seq")
    cfg_pos = lax.axis_index("cfg")
    prompts = image_tokens.shape[0]
    image_rows = image_tokens.shape[1]
    text_rows = text_tokens.shape[2]
    local_len = text_rows + image_rows
    dim_local = image_tokens.shape[2]
    dim_seq = pooled_vector.shape[1]
    heads_local = qkv_weight.shape[2]
    row_count = prompts * local_len
    sigma_now, step_size = plan(timestep)
    embedded = lax.dynamic_slice_in_dim(time_embedding(sigma_now, D), seq_pos * dim_seq, dim_seq)
    cond_vec = jax.nn.silu(pooled_vector[0] + embedded).astype(jnp.bfloat16)[None]
    mod_terms = jnp.dot(
        cond_vec, mod_weight.reshape(dim_seq, 3 * dim_local), preferred_element_type=jnp.float32
    )
    seq_count = lax.psum(1, "seq")
    mod_spread = jnp.broadcast_to(mod_terms.reshape(1, 3, dim_local), (seq_count, 3, dim_local))
    modulation = jnp.sum(lax.all_to_all(mod_spread, "seq", 0, 0, tiled=True), axis=0)
    local_rows = jnp.concatenate([text_tokens[0], image_tokens], axis=1)
    hidden = local_rows.astype(jnp.float32)
    totals, squares = lax.psum(
        (jnp.sum(hidden, axis=-1), jnp.sum(hidden * hidden, axis=-1)), "wblk"
    )
    average = (totals / D)[..., None]
    variance = (squares / D)[..., None] - average * average
    normed = (
        (hidden - average) * lax.rsqrt(variance + epsilon) * (1.0 + modulation[1]) + modulation[0]
    ).astype(jnp.bfloat16)
    width_rows = qkv_weight.shape[0]
    qkv_cols = 3 * heads_local * HD
    qkv_full = lax.all_gather(
        qkv_weight.reshape(width_rows, qkv_cols), "seq", axis=0, tiled=True
    )
    wblk_count = lax.psum(1, "wblk")
    spread = jnp.broadcast_to(normed.reshape(1, row_count, dim_local), (wblk_count, row_count, dim_local))
    gathered = lax.all_to_all(spread, "wblk", 0, 0, tiled=True)
    up_cols = up_weight.shape[1]
    tail_source = jnp.concatenate(
        [up_weight, jnp.concatenate([attn_weight, down_weight], axis=0).T], axis=1
    )
    tail_source, gathered = lax.optimization_barrier((tail_source, gathered))
    tail_full = lax.all_gather(tail_source, "seq", axis=0, tiled=True)
    up_full = tail_full[:, :up_cols]
    projected = jnp.einsum(
        "wrf,wfn->rn",
        gathered,
        qkv_full.reshape(wblk_count, dim_local, -1),
        preferred_element_type=jnp.float32,
    )
    mlp_units = jnp.einsum(
        "wrf,wfn->rn",
        gathered,
        up_full.reshape(wblk_count, dim_local, -1),
        preferred_element_type=jnp.float32,
    )
    projected = projected.reshape(prompts, local_len, 3, heads_local, HD)
    image_index = seq_pos * image_rows + jnp.arange(image_rows, dtype=jnp.int32)
    height_pos = jnp.concatenate(
        [jnp.zeros((text_rows,), jnp.float32), (image_index // GRID).astype(jnp.float32)]
    )
    width_pos = jnp.concatenate(
        [jnp.zeros((text_rows,), jnp.float32), (image_index % GRID).astype(jnp.float32)]
    )
    angles = rotary_angles(height_pos, width_pos)
    queries = rotate(head_norm(projected[:, :, 0], query_gain), angles).astype(jnp.bfloat16)
    key_rows = rotate(head_norm(projected[:, :, 1], key_gain), angles).astype(jnp.bfloat16)
    values = projected[:, :, 2].astype(jnp.bfloat16)
    scale_factor = HD ** (-0.5)
    pair_count = prompts * heads_local
    subs = seq_count // pair_count
    sub_rows = local_len // subs
    pair_keys = key_rows.transpose(0, 2, 1, 3).reshape(pair_count, local_len, HD)
    pair_values = values.transpose(0, 2, 1, 3).reshape(pair_count, local_len, HD)
    pair_queries = queries.transpose(0, 2, 1, 3).reshape(seq_count, sub_rows, HD)
    send = jnp.concatenate(
        [
            jnp.broadcast_to(pair_keys[:, None], (pair_count, subs, local_len, HD)).reshape(
                seq_count, local_len, HD
            ),
            jnp.broadcast_to(pair_values[:, None], (pair_count, subs, local_len, HD)).reshape(
                seq_count, local_len, HD
            ),
            pair_queries,
        ],
        axis=1,
    )
    received = lax.all_to_all(send, "seq", 0, 0, tiled=True)
    key_piece = received[:, :local_len].reshape(seq_count * local_len, HD)
    value_piece = received[:, local_len : 2 * local_len].reshape(seq_count * local_len, HD)
    query_piece = received[:, 2 * local_len :].reshape(seq_count * sub_rows, HD)
    my_prompt = seq_pos // subs // heads_local
    width_keys = key_piece.shape[0]
    where_global = jnp.arange(width_keys, dtype=jnp.int32)
    shard_index = where_global // local_len
    within = where_global % local_len
    text_index = shard_index * text_rows + within
    key_live = (within >= text_rows) | (text_index < lengths[my_prompt])
    scores = (
        jnp.dot(query_piece, key_piece.T, preferred_element_type=jnp.float32) * scale_factor
    )
    scores = jnp.where(key_live[None, :], scores, -1e30)
    top_score = jnp.max(scores, axis=-1, keepdims=True)
    weights = jnp.exp(scores - top_score)
    denominator = jnp.sum(weights, axis=-1, keepdims=True)
    numerator = jnp.dot(
        weights.astype(jnp.bfloat16), value_piece, preferred_element_type=jnp.float32
    )
    mixed = (numerator / denominator).astype(jnp.bfloat16).reshape(seq_count, sub_rows, HD)
    returned = lax.all_to_all(mixed, "seq", 0, 0, tiled=True)
    attended = returned.reshape(prompts, heads_local, local_len, HD)
    attended = attended.transpose(0, 2, 1, 3).reshape(row_count, heads_local * HD)
    activated = jax.nn.gelu(mlp_units, approximate=True).astype(jnp.bfloat16)
    block_terms = jnp.einsum(
        "bjk,rk->brj",
        tail_full[:, up_cols:].reshape(wblk_count, dim_local, -1),
        jnp.concatenate([attended, activated], axis=1),
        preferred_element_type=jnp.float32,
    )
    branch = lax.psum_scatter(
        block_terms.astype(jnp.bfloat16), "wblk", scatter_dimension=0, tiled=True
    )
    branch = branch.reshape(prompts, local_len, dim_local).astype(jnp.float32)
    layer_out = hidden + modulation[2] * branch
    text_out = layer_out[:, :text_rows].astype(jnp.bfloat16)[None]
    image_out = layer_out[:, text_rows:]
    own_prompts = prompts // 2
    rounded_out = image_out.astype(jnp.bfloat16)
    kept = lax.dynamic_slice_in_dim(rounded_out, cfg_pos * own_prompts, own_prompts, 0)
    given = lax.dynamic_slice_in_dim(rounded_out, (1 - cfg_pos) * own_prompts, own_prompts, 0)
    taken = lax.ppermute(given, "cfg", [(0, 1), (1, 0)]).astype(jnp.float32)
    kept = kept.astype(jnp.float32)
    conditional = jnp.where(cfg_pos == 0, kept, taken)
    unconditional = jnp.where(cfg_pos == 0, taken, kept)
    velocity = unconditional + guidance * (conditional - unconditional)
    latent = lax.dynamic_slice_in_dim(image_tokens, cfg_pos * own_prompts, own_prompts, 0).astype(
        jnp.float32
    )
    new_image = latent + step_size * velocity
    return (text_out, velocity, new_image)


def solution(mesh):
    in_specs = (
        P("cfg", None, "seq", "wblk"),
        P(None, "seq", "wblk"),
        P("cfg", "seq"),
        P("seq", None, "wblk"),
        P("seq", None, "wblk", None),
        P("seq", "wblk"),
        P(),
        P(),
        P("wblk", "seq"),
        P("wblk", "seq"),
        P(),
        P(),
    )
    out_specs = (P("cfg", None, "seq", "wblk"), P("cfg", "seq", "wblk"), P("cfg", "seq", "wblk"))
    return jax.shard_map(shards, mesh=mesh, in_specs=in_specs, out_specs=out_specs, check_vma=False)
```

```python
import math

import jax
import jax.numpy as jnp
from jax import lax
from jax.sharding import PartitionSpec as P

D = 3072
HD = 128
GRID = 64
STEPS = 28


epsilon = 1e-06
guidance = 3.5
time_shift = 3.0
rope_theta = 10000.0


def plan(timestep):
    step_index = timestep[0].astype(jnp.float32)
    time_now = 1.0 - step_index / STEPS
    time_next = 1.0 - (step_index + 1.0) / STEPS
    sigma_now = time_shift * time_now / (1.0 + (time_shift - 1.0) * time_now)
    sigma_next = time_shift * time_next / (1.0 + (time_shift - 1.0) * time_next)
    return (sigma_now, sigma_next - sigma_now)


def time_embedding(sigma_now, dim_count):
    halfwidth = dim_count // 2
    frequency = jnp.exp(-math.log(10000.0) * jnp.arange(halfwidth, dtype=jnp.float32) / halfwidth)
    angles = 1000.0 * sigma_now * frequency
    return jnp.concatenate([jnp.cos(angles), jnp.sin(angles)])


def inverse_freq(dim_count):
    return rope_theta ** (-jnp.arange(0, dim_count, 2, dtype=jnp.float32) / dim_count)


def rotary_angles(height_pos, width_pos):
    still_dims = HD // 8
    axis_dims = (HD - still_dims) // 2
    return jnp.concatenate(
        [
            jnp.zeros((height_pos.shape[0], still_dims // 2), jnp.float32),
            height_pos[:, None] * inverse_freq(axis_dims)[None],
            width_pos[:, None] * inverse_freq(axis_dims)[None],
        ],
        axis=1,
    )


def rotate(vectors, angles):
    paired_dims = vectors.reshape(vectors.shape[:-1] + (HD // 2, 2))
    cosine_table = jnp.cos(angles)[:, None, :]
    sine_table = jnp.sin(angles)[:, None, :]
    first_part = paired_dims[..., 0]
    second_part = paired_dims[..., 1]
    turned = jnp.stack(
        [
            first_part * cosine_table - second_part * sine_table,
            first_part * sine_table + second_part * cosine_table,
        ],
        axis=-1,
    )
    return turned.reshape(vectors.shape)


def head_norm(vectors, gain_vector):
    return (
        vectors
        * lax.rsqrt(jnp.mean(vectors * vectors, axis=-1, keepdims=True) + epsilon)
        * gain_vector
    )


def input_folder(source, pieces):
    width_rows = pieces[0].shape[0]
    first_total = jnp.dot(
        source, pieces[0].reshape(width_rows, -1), preferred_element_type=jnp.float32
    )
    second_total = jnp.dot(source, pieces[1], preferred_element_type=jnp.float32)
    return (first_total, second_total)


def output_folder(attended, activated, pieces):
    block_cols = jnp.dot(attended, pieces[0], preferred_element_type=jnp.float32)
    block_cols = block_cols + jnp.dot(activated, pieces[1], preferred_element_type=jnp.float32)
    return block_cols


def shards(
    text_tokens,
    image_tokens,
    pooled_vector,
    mod_weight,
    qkv_weight,
    up_weight,
    query_gain,
    key_gain,
    attn_weight,
    down_weight,
    lengths,
    timestep,
):
    seq_pos = lax.axis_index("seq")
    cfg_pos = lax.axis_index("cfg")
    prompts = image_tokens.shape[0]
    image_rows = image_tokens.shape[1]
    text_rows = text_tokens.shape[2]
    local_len = text_rows + image_rows
    dim_local = image_tokens.shape[2]
    dim_seq = pooled_vector.shape[1]
    heads_local = qkv_weight.shape[2]
    row_count = prompts * local_len
    sigma_now, step_size = plan(timestep)
    embedded = lax.dynamic_slice_in_dim(time_embedding(sigma_now, D), seq_pos * dim_seq, dim_seq)
    cond_vec = jax.nn.silu(pooled_vector[0] + embedded).astype(jnp.bfloat16)[None]
    mod_terms = jnp.dot(
        cond_vec, mod_weight.reshape(dim_seq, 3 * dim_local), preferred_element_type=jnp.float32
    )
    seq_count = lax.psum(1, "seq")
    mod_spread = jnp.broadcast_to(mod_terms.reshape(1, 3, dim_local), (seq_count, 3, dim_local))
    modulation = jnp.sum(lax.all_to_all(mod_spread, "seq", 0, 0, tiled=True), axis=0)
    local_rows = jnp.concatenate([text_tokens[0], image_tokens], axis=1)
    hidden = local_rows.astype(jnp.float32)
    totals, squares = lax.psum(
        (jnp.sum(hidden, axis=-1), jnp.sum(hidden * hidden, axis=-1)), "wblk"
    )
    average = (totals / D)[..., None]
    variance = (squares / D)[..., None] - average * average
    normed = (
        (hidden - average) * lax.rsqrt(variance + epsilon) * (1.0 + modulation[1]) + modulation[0]
    ).astype(jnp.bfloat16)
    width_rows = qkv_weight.shape[0]
    qkv_cols = 3 * heads_local * HD
    qkv_full = lax.all_gather(
        qkv_weight.reshape(width_rows, qkv_cols), "seq", axis=0, tiled=True
    )
    wblk_count = lax.psum(1, "wblk")
    spread = jnp.broadcast_to(normed.reshape(1, row_count, dim_local), (wblk_count, row_count, dim_local))
    gathered = lax.all_to_all(spread, "wblk", 0, 0, tiled=True)
    up_cols = up_weight.shape[1]
    tail_source = jnp.concatenate(
        [up_weight, jnp.concatenate([attn_weight, down_weight], axis=0).T], axis=1
    )
    tail_source, gathered = lax.optimization_barrier((tail_source, gathered))
    tail_full = lax.all_gather(tail_source, "seq", axis=0, tiled=True)
    up_full, out_weight_t = lax.optimization_barrier(
        (tail_full[:, :up_cols], tail_full[:, up_cols:])
    )
    projected = jnp.einsum(
        "wrf,wfn->rn",
        gathered,
        qkv_full.reshape(wblk_count, dim_local, -1),
        preferred_element_type=jnp.float32,
    )
    mlp_units = jnp.einsum(
        "wrf,wfn->rn",
        gathered,
        up_full.reshape(wblk_count, dim_local, -1),
        preferred_element_type=jnp.float32,
    )
    projected = projected.reshape(prompts, local_len, 3, heads_local, HD)
    image_index = seq_pos * image_rows + jnp.arange(image_rows, dtype=jnp.int32)
    height_pos = jnp.concatenate(
        [jnp.zeros((text_rows,), jnp.float32), (image_index // GRID).astype(jnp.float32)]
    )
    width_pos = jnp.concatenate(
        [jnp.zeros((text_rows,), jnp.float32), (image_index % GRID).astype(jnp.float32)]
    )
    angles = rotary_angles(height_pos, width_pos)
    queries = rotate(head_norm(projected[:, :, 0], query_gain), angles).astype(jnp.bfloat16)
    key_rows = rotate(head_norm(projected[:, :, 1], key_gain), angles).astype(jnp.bfloat16)
    values = projected[:, :, 2].astype(jnp.bfloat16)
    scale_factor = HD ** (-0.5)
    pair_count = prompts * heads_local
    subs = seq_count // pair_count
    sub_rows = local_len // subs
    pair_keys = key_rows.transpose(0, 2, 1, 3).reshape(pair_count, local_len, HD)
    pair_values = values.transpose(0, 2, 1, 3).reshape(pair_count, local_len, HD)
    pair_queries = queries.transpose(0, 2, 1, 3).reshape(seq_count, sub_rows, HD)
    send = jnp.concatenate(
        [
            jnp.broadcast_to(pair_keys[:, None], (pair_count, subs, local_len, HD)).reshape(
                seq_count, local_len, HD
            ),
            jnp.broadcast_to(pair_values[:, None], (pair_count, subs, local_len, HD)).reshape(
                seq_count, local_len, HD
            ),
            pair_queries,
        ],
        axis=1,
    )
    received = lax.all_to_all(send, "seq", 0, 0, tiled=True)
    key_piece = received[:, :local_len].reshape(seq_count * local_len, HD)
    value_piece = received[:, local_len : 2 * local_len].reshape(seq_count * local_len, HD)
    query_piece = received[:, 2 * local_len :].reshape(seq_count * sub_rows, HD)
    my_prompt = seq_pos // subs // heads_local
    width_keys = key_piece.shape[0]
    where_global = jnp.arange(width_keys, dtype=jnp.int32)
    shard_index = where_global // local_len
    within = where_global % local_len
    text_index = shard_index * text_rows + within
    key_live = (within >= text_rows) | (text_index < lengths[my_prompt])
    scores = (
        jnp.dot(query_piece, key_piece.T, preferred_element_type=jnp.float32) * scale_factor
    )
    scores = jnp.where(key_live[None, :], scores, -1e30)
    top_score = jnp.max(scores, axis=-1, keepdims=True)
    weights = jnp.exp(scores - top_score)
    denominator = jnp.sum(weights, axis=-1, keepdims=True)
    numerator = jnp.dot(
        weights.astype(jnp.bfloat16), value_piece, preferred_element_type=jnp.float32
    )
    mixed = (numerator / denominator).astype(jnp.bfloat16).reshape(seq_count, sub_rows, HD)
    returned = lax.all_to_all(mixed, "seq", 0, 0, tiled=True)
    attended = returned.reshape(prompts, heads_local, local_len, HD)
    attended = attended.transpose(0, 2, 1, 3).reshape(row_count, heads_local * HD)
    activated = jax.nn.gelu(mlp_units, approximate=True).astype(jnp.bfloat16)
    block_terms = jnp.einsum(
        "bjk,rk->brj",
        out_weight_t.reshape(wblk_count, dim_local, -1),
        jnp.concatenate([attended, activated], axis=1),
        preferred_element_type=jnp.float32,
    )
    branch = lax.psum_scatter(
        block_terms.astype(jnp.bfloat16), "wblk", scatter_dimension=0, tiled=True
    )
    branch = branch.reshape(prompts, local_len, dim_local).astype(jnp.float32)
    layer_out = hidden + modulation[2] * branch
    text_out = layer_out[:, :text_rows].astype(jnp.bfloat16)[None]
    image_out = layer_out[:, text_rows:]
    own_prompts = prompts // 2
    rounded_out = image_out.astype(jnp.bfloat16)
    kept = lax.dynamic_slice_in_dim(rounded_out, cfg_pos * own_prompts, own_prompts, 0)
    given = lax.dynamic_slice_in_dim(rounded_out, (1 - cfg_pos) * own_prompts, own_prompts, 0)
    taken = lax.ppermute(given, "cfg", [(0, 1), (1, 0)]).astype(jnp.float32)
    kept = kept.astype(jnp.float32)
    conditional = jnp.where(cfg_pos == 0, kept, taken)
    unconditional = jnp.where(cfg_pos == 0, taken, kept)
    velocity = unconditional + guidance * (conditional - unconditional)
    latent = lax.dynamic_slice_in_dim(image_tokens, cfg_pos * own_prompts, own_prompts, 0).astype(
        jnp.float32
    )
    new_image = latent + step_size * velocity
    return (text_out, velocity, new_image)


def solution(mesh):
    in_specs = (
        P("cfg", None, "seq", "wblk"),
        P(None, "seq", "wblk"),
        P("cfg", "seq"),
        P("seq", None, "wblk"),
        P("seq", None, "wblk", None),
        P("seq", "wblk"),
        P(),
        P(),
        P("wblk", "seq"),
        P("wblk", "seq"),
        P(),
        P(),
    )
    out_specs = (P("cfg", None, "seq", "wblk"), P("cfg", "seq", "wblk"), P("cfg", "seq", "wblk"))
    return jax.shard_map(shards, mesh=mesh, in_specs=in_specs, out_specs=out_specs, check_vma=False)
```

```python
import math

import jax
import jax.numpy as jnp
from jax import lax
from jax.sharding import PartitionSpec as P

D = 3072
HD = 128
GRID = 64
STEPS = 28


epsilon = 1e-06
guidance = 3.5
time_shift = 3.0
rope_theta = 10000.0


def plan(timestep):
    step_index = timestep[0].astype(jnp.float32)
    time_now = 1.0 - step_index / STEPS
    time_next = 1.0 - (step_index + 1.0) / STEPS
    sigma_now = time_shift * time_now / (1.0 + (time_shift - 1.0) * time_now)
    sigma_next = time_shift * time_next / (1.0 + (time_shift - 1.0) * time_next)
    return (sigma_now, sigma_next - sigma_now)


def time_embedding(sigma_now, dim_count):
    halfwidth = dim_count // 2
    frequency = jnp.exp(-math.log(10000.0) * jnp.arange(halfwidth, dtype=jnp.float32) / halfwidth)
    angles = 1000.0 * sigma_now * frequency
    return jnp.concatenate([jnp.cos(angles), jnp.sin(angles)])


def inverse_freq(dim_count):
    return rope_theta ** (-jnp.arange(0, dim_count, 2, dtype=jnp.float32) / dim_count)


def rotary_angles(height_pos, width_pos):
    still_dims = HD // 8
    axis_dims = (HD - still_dims) // 2
    return jnp.concatenate(
        [
            jnp.zeros((height_pos.shape[0], still_dims // 2), jnp.float32),
            height_pos[:, None] * inverse_freq(axis_dims)[None],
            width_pos[:, None] * inverse_freq(axis_dims)[None],
        ],
        axis=1,
    )


def rotate(vectors, angles):
    paired_dims = vectors.reshape(vectors.shape[:-1] + (HD // 2, 2))
    cosine_table = jnp.cos(angles)[:, None, :]
    sine_table = jnp.sin(angles)[:, None, :]
    first_part = paired_dims[..., 0]
    second_part = paired_dims[..., 1]
    turned = jnp.stack(
        [
            first_part * cosine_table - second_part * sine_table,
            first_part * sine_table + second_part * cosine_table,
        ],
        axis=-1,
    )
    return turned.reshape(vectors.shape)


def head_norm(vectors, gain_vector):
    return (
        vectors
        * lax.rsqrt(jnp.mean(vectors * vectors, axis=-1, keepdims=True) + epsilon)
        * gain_vector
    )


def input_folder(source, pieces):
    width_rows = pieces[0].shape[0]
    first_total = jnp.dot(
        source, pieces[0].reshape(width_rows, -1), preferred_element_type=jnp.float32
    )
    second_total = jnp.dot(source, pieces[1], preferred_element_type=jnp.float32)
    return (first_total, second_total)


def output_folder(attended, activated, pieces):
    block_cols = jnp.dot(attended, pieces[0], preferred_element_type=jnp.float32)
    block_cols = block_cols + jnp.dot(activated, pieces[1], preferred_element_type=jnp.float32)
    return block_cols


def shards(
    text_tokens,
    image_tokens,
    pooled_vector,
    mod_weight,
    qkv_weight,
    up_weight,
    query_gain,
    key_gain,
    attn_weight,
    down_weight,
    lengths,
    timestep,
):
    seq_pos = lax.axis_index("seq")
    cfg_pos = lax.axis_index("cfg")
    prompts = image_tokens.shape[0]
    image_rows = image_tokens.shape[1]
    text_rows = text_tokens.shape[2]
    local_len = text_rows + image_rows
    dim_local = image_tokens.shape[2]
    dim_seq = pooled_vector.shape[1]
    heads_local = qkv_weight.shape[2]
    row_count = prompts * local_len
    sigma_now, step_size = plan(timestep)
    embedded = lax.dynamic_slice_in_dim(time_embedding(sigma_now, D), seq_pos * dim_seq, dim_seq)
    cond_vec = jax.nn.silu(pooled_vector[0] + embedded).astype(jnp.bfloat16)[None]
    mod_terms = jnp.dot(
        cond_vec, mod_weight.reshape(dim_seq, 3 * dim_local), preferred_element_type=jnp.float32
    )
    seq_count = lax.psum(1, "seq")
    mod_spread = jnp.broadcast_to(mod_terms.reshape(1, 3, dim_local), (seq_count, 3, dim_local))
    modulation = jnp.sum(lax.all_to_all(mod_spread, "seq", 0, 0, tiled=True), axis=0)
    local_rows = jnp.concatenate([text_tokens[0], image_tokens], axis=1)
    hidden = local_rows.astype(jnp.float32)
    totals, squares = lax.psum(
        (jnp.sum(hidden, axis=-1), jnp.sum(hidden * hidden, axis=-1)), "wblk"
    )
    average = (totals / D)[..., None]
    variance = (squares / D)[..., None] - average * average
    normed = (
        (hidden - average) * lax.rsqrt(variance + epsilon) * (1.0 + modulation[1]) + modulation[0]
    ).astype(jnp.bfloat16)
    width_rows = qkv_weight.shape[0]
    qkv_cols = 3 * heads_local * HD
    qkv_full = lax.all_gather(
        qkv_weight.reshape(width_rows, qkv_cols), "seq", axis=0, tiled=True
    )
    wblk_count = lax.psum(1, "wblk")
    spread = jnp.broadcast_to(normed.reshape(row_count, 1, dim_local), (row_count, wblk_count, dim_local))
    gathered = lax.all_to_all(spread, "wblk", 1, 1, tiled=True).reshape(row_count, D)
    up_cols = up_weight.shape[1]
    tail_source = jnp.concatenate(
        [up_weight, jnp.concatenate([attn_weight, down_weight], axis=0).T], axis=1
    )
    tail_source, gathered = lax.optimization_barrier((tail_source, gathered))
    tail_full = lax.all_gather(tail_source, "seq", axis=0, tiled=True)
    up_full, out_weight_t = lax.optimization_barrier(
        (tail_full[:, :up_cols], tail_full[:, up_cols:])
    )
    projected = jnp.einsum(
        "rk,kn->rn",
        gathered,
        qkv_full,
        preferred_element_type=jnp.float32,
    )
    mlp_units = jnp.einsum(
        "rk,kn->rn",
        gathered,
        up_full,
        preferred_element_type=jnp.float32,
    )
    projected = projected.reshape(prompts, local_len, 3, heads_local, HD)
    image_index = seq_pos * image_rows + jnp.arange(image_rows, dtype=jnp.int32)
    height_pos = jnp.concatenate(
        [jnp.zeros((text_rows,), jnp.float32), (image_index // GRID).astype(jnp.float32)]
    )
    width_pos = jnp.concatenate(
        [jnp.zeros((text_rows,), jnp.float32), (image_index % GRID).astype(jnp.float32)]
    )
    angles = rotary_angles(height_pos, width_pos)
    queries = rotate(head_norm(projected[:, :, 0], query_gain), angles).astype(jnp.bfloat16)
    key_rows = rotate(head_norm(projected[:, :, 1], key_gain), angles).astype(jnp.bfloat16)
    values = projected[:, :, 2].astype(jnp.bfloat16)
    scale_factor = HD ** (-0.5)
    pair_count = prompts * heads_local
    subs = seq_count // pair_count
    sub_rows = local_len // subs
    pair_keys = key_rows.transpose(0, 2, 1, 3).reshape(pair_count, local_len, HD)
    pair_values = values.transpose(0, 2, 1, 3).reshape(pair_count, local_len, HD)
    pair_queries = queries.transpose(0, 2, 1, 3).reshape(seq_count, sub_rows, HD)
    send = jnp.concatenate(
        [
            jnp.broadcast_to(pair_keys[:, None], (pair_count, subs, local_len, HD)).reshape(
                seq_count, local_len, HD
            ),
            jnp.broadcast_to(pair_values[:, None], (pair_count, subs, local_len, HD)).reshape(
                seq_count, local_len, HD
            ),
            pair_queries,
        ],
        axis=1,
    )
    received = lax.all_to_all(send, "seq", 0, 0, tiled=True)
    key_piece = received[:, :local_len].reshape(seq_count * local_len, HD)
    value_piece = received[:, local_len : 2 * local_len].reshape(seq_count * local_len, HD)
    query_piece = received[:, 2 * local_len :].reshape(seq_count * sub_rows, HD)
    my_prompt = seq_pos // subs // heads_local
    width_keys = key_piece.shape[0]
    where_global = jnp.arange(width_keys, dtype=jnp.int32)
    shard_index = where_global // local_len
    within = where_global % local_len
    text_index = shard_index * text_rows + within
    key_live = (within >= text_rows) | (text_index < lengths[my_prompt])
    scores = (
        jnp.dot(query_piece, key_piece.T, preferred_element_type=jnp.float32) * scale_factor
    )
    scores = jnp.where(key_live[None, :], scores, -1e30)
    top_score = jnp.max(scores, axis=-1, keepdims=True)
    weights = jnp.exp(scores - top_score)
    denominator = jnp.sum(weights, axis=-1, keepdims=True)
    numerator = jnp.dot(
        weights.astype(jnp.bfloat16), value_piece, preferred_element_type=jnp.float32
    )
    mixed = (numerator / denominator).astype(jnp.bfloat16).reshape(seq_count, sub_rows, HD)
    returned = lax.all_to_all(mixed, "seq", 0, 0, tiled=True)
    attended = returned.reshape(prompts, heads_local, local_len, HD)
    attended = attended.transpose(0, 2, 1, 3).reshape(row_count, heads_local * HD)
    activated = jax.nn.gelu(mlp_units, approximate=True).astype(jnp.bfloat16)
    block_terms = jnp.einsum(
        "bjk,rk->brj",
        out_weight_t.reshape(wblk_count, dim_local, -1),
        jnp.concatenate([attended, activated], axis=1),
        preferred_element_type=jnp.float32,
    )
    branch = lax.psum_scatter(
        block_terms.astype(jnp.bfloat16), "wblk", scatter_dimension=0, tiled=True
    )
    branch = branch.reshape(prompts, local_len, dim_local).astype(jnp.float32)
    layer_out = hidden + modulation[2] * branch
    text_out = layer_out[:, :text_rows].astype(jnp.bfloat16)[None]
    image_out = layer_out[:, text_rows:]
    own_prompts = prompts // 2
    rounded_out = image_out.astype(jnp.bfloat16)
    kept = lax.dynamic_slice_in_dim(rounded_out, cfg_pos * own_prompts, own_prompts, 0)
    given = lax.dynamic_slice_in_dim(rounded_out, (1 - cfg_pos) * own_prompts, own_prompts, 0)
    taken = lax.ppermute(given, "cfg", [(0, 1), (1, 0)]).astype(jnp.float32)
    kept = kept.astype(jnp.float32)
    conditional = jnp.where(cfg_pos == 0, kept, taken)
    unconditional = jnp.where(cfg_pos == 0, taken, kept)
    velocity = unconditional + guidance * (conditional - unconditional)
    latent = lax.dynamic_slice_in_dim(image_tokens, cfg_pos * own_prompts, own_prompts, 0).astype(
        jnp.float32
    )
    new_image = latent + step_size * velocity
    return (text_out, velocity, new_image)


def solution(mesh):
    in_specs = (
        P("cfg", None, "seq", "wblk"),
        P(None, "seq", "wblk"),
        P("cfg", "seq"),
        P("seq", None, "wblk"),
        P("seq", None, "wblk", None),
        P("seq", "wblk"),
        P(),
        P(),
        P("wblk", "seq"),
        P("wblk", "seq"),
        P(),
        P(),
    )
    out_specs = (P("cfg", None, "seq", "wblk"), P("cfg", "seq", "wblk"), P("cfg", "seq", "wblk"))
    return jax.shard_map(shards, mesh=mesh, in_specs=in_specs, out_specs=out_specs, check_vma=False)
```

```python
import math

import jax
import jax.numpy as jnp
from jax import lax
from jax.sharding import PartitionSpec as P

D = 3072
HD = 128
GRID = 64
STEPS = 28


epsilon = 1e-06
guidance = 3.5
time_shift = 3.0
rope_theta = 10000.0


def plan(timestep):
    step_index = timestep[0].astype(jnp.float32)
    time_now = 1.0 - step_index / STEPS
    time_next = 1.0 - (step_index + 1.0) / STEPS
    sigma_now = time_shift * time_now / (1.0 + (time_shift - 1.0) * time_now)
    sigma_next = time_shift * time_next / (1.0 + (time_shift - 1.0) * time_next)
    return (sigma_now, sigma_next - sigma_now)


def time_embedding(sigma_now, dim_count):
    halfwidth = dim_count // 2
    frequency = jnp.exp(-math.log(10000.0) * jnp.arange(halfwidth, dtype=jnp.float32) / halfwidth)
    angles = 1000.0 * sigma_now * frequency
    return jnp.concatenate([jnp.cos(angles), jnp.sin(angles)])


def inverse_freq(dim_count):
    return rope_theta ** (-jnp.arange(0, dim_count, 2, dtype=jnp.float32) / dim_count)


def rotary_angles(height_pos, width_pos):
    still_dims = HD // 8
    axis_dims = (HD - still_dims) // 2
    return jnp.concatenate(
        [
            jnp.zeros((height_pos.shape[0], still_dims // 2), jnp.float32),
            height_pos[:, None] * inverse_freq(axis_dims)[None],
            width_pos[:, None] * inverse_freq(axis_dims)[None],
        ],
        axis=1,
    )


def rotate(vectors, angles):
    paired_dims = vectors.reshape(vectors.shape[:-1] + (HD // 2, 2))
    cosine_table = jnp.cos(angles)[:, None, :]
    sine_table = jnp.sin(angles)[:, None, :]
    first_part = paired_dims[..., 0]
    second_part = paired_dims[..., 1]
    turned = jnp.stack(
        [
            first_part * cosine_table - second_part * sine_table,
            first_part * sine_table + second_part * cosine_table,
        ],
        axis=-1,
    )
    return turned.reshape(vectors.shape)


def head_norm(vectors, gain_vector):
    return (
        vectors
        * lax.rsqrt(jnp.mean(vectors * vectors, axis=-1, keepdims=True) + epsilon)
        * gain_vector
    )


def input_folder(source, pieces):
    width_rows = pieces[0].shape[0]
    first_total = jnp.dot(
        source, pieces[0].reshape(width_rows, -1), preferred_element_type=jnp.float32
    )
    second_total = jnp.dot(source, pieces[1], preferred_element_type=jnp.float32)
    return (first_total, second_total)


def output_folder(attended, activated, pieces):
    block_cols = jnp.dot(attended, pieces[0], preferred_element_type=jnp.float32)
    block_cols = block_cols + jnp.dot(activated, pieces[1], preferred_element_type=jnp.float32)
    return block_cols


def shards(
    text_tokens,
    image_tokens,
    pooled_vector,
    mod_weight,
    qkv_weight,
    up_weight,
    query_gain,
    key_gain,
    attn_weight,
    down_weight,
    lengths,
    timestep,
):
    seq_pos = lax.axis_index("seq")
    cfg_pos = lax.axis_index("cfg")
    prompts = image_tokens.shape[0]
    image_rows = image_tokens.shape[1]
    text_rows = text_tokens.shape[2]
    local_len = text_rows + image_rows
    dim_local = image_tokens.shape[2]
    dim_seq = pooled_vector.shape[1]
    heads_local = qkv_weight.shape[2]
    row_count = prompts * local_len
    sigma_now, step_size = plan(timestep)
    embedded = lax.dynamic_slice_in_dim(time_embedding(sigma_now, D), seq_pos * dim_seq, dim_seq)
    cond_vec = jax.nn.silu(pooled_vector[0] + embedded).astype(jnp.bfloat16)[None]
    mod_terms = jnp.dot(
        cond_vec, mod_weight.reshape(dim_seq, 3 * dim_local), preferred_element_type=jnp.float32
    )
    seq_count = lax.psum(1, "seq")
    mod_spread = jnp.broadcast_to(mod_terms.reshape(1, 3, dim_local), (seq_count, 3, dim_local))
    modulation = jnp.sum(lax.all_to_all(mod_spread, "seq", 0, 0, tiled=True), axis=0)
    local_rows = jnp.concatenate([text_tokens[0], image_tokens], axis=1)
    hidden = local_rows.astype(jnp.float32)
    totals, squares = lax.psum(
        (jnp.sum(hidden, axis=-1), jnp.sum(hidden * hidden, axis=-1)), "wblk"
    )
    average = (totals / D)[..., None]
    variance = (squares / D)[..., None] - average * average
    normed = (
        (hidden - average) * lax.rsqrt(variance + epsilon) * (1.0 + modulation[1]) + modulation[0]
    ).astype(jnp.bfloat16)
    width_rows = qkv_weight.shape[0]
    qkv_cols = 3 * heads_local * HD
    head_full = lax.all_gather(
        jnp.concatenate([qkv_weight.reshape(width_rows, qkv_cols), attn_weight.T], axis=1),
        "seq",
        axis=0,
        tiled=True,
    )
    qkv_full, attn_weight_t = lax.optimization_barrier(
        (head_full[:, :qkv_cols], head_full[:, qkv_cols:])
    )
    wblk_count = lax.psum(1, "wblk")
    spread = jnp.broadcast_to(normed.reshape(row_count, 1, dim_local), (row_count, wblk_count, dim_local))
    gathered = lax.all_to_all(spread, "wblk", 1, 1, tiled=True).reshape(row_count, D)
    up_cols = up_weight.shape[1]
    tail_source = jnp.concatenate([up_weight, down_weight.T], axis=1)
    tail_source, gathered = lax.optimization_barrier((tail_source, gathered))
    tail_full = lax.all_gather(tail_source, "seq", axis=0, tiled=True)
    up_full, out_weight_t = lax.optimization_barrier(
        (tail_full[:, :up_cols], tail_full[:, up_cols:])
    )
    projected = jnp.einsum(
        "rk,kn->rn",
        gathered,
        qkv_full,
        preferred_element_type=jnp.float32,
    )
    mlp_units = jnp.einsum(
        "rk,kn->rn",
        gathered,
        up_full,
        preferred_element_type=jnp.float32,
    )
    projected = projected.reshape(prompts, local_len, 3, heads_local, HD)
    image_index = seq_pos * image_rows + jnp.arange(image_rows, dtype=jnp.int32)
    height_pos = jnp.concatenate(
        [jnp.zeros((text_rows,), jnp.float32), (image_index // GRID).astype(jnp.float32)]
    )
    width_pos = jnp.concatenate(
        [jnp.zeros((text_rows,), jnp.float32), (image_index % GRID).astype(jnp.float32)]
    )
    angles = rotary_angles(height_pos, width_pos)
    queries = rotate(head_norm(projected[:, :, 0], query_gain), angles).astype(jnp.bfloat16)
    key_rows = rotate(head_norm(projected[:, :, 1], key_gain), angles).astype(jnp.bfloat16)
    values = projected[:, :, 2].astype(jnp.bfloat16)
    scale_factor = HD ** (-0.5)
    pair_count = prompts * heads_local
    subs = seq_count // pair_count
    sub_rows = local_len // subs
    pair_keys = key_rows.transpose(0, 2, 1, 3).reshape(pair_count, local_len, HD)
    pair_values = values.transpose(0, 2, 1, 3).reshape(pair_count, local_len, HD)
    pair_queries = queries.transpose(0, 2, 1, 3).reshape(seq_count, sub_rows, HD)
    send = jnp.concatenate(
        [
            jnp.broadcast_to(pair_keys[:, None], (pair_count, subs, local_len, HD)).reshape(
                seq_count, local_len, HD
            ),
            jnp.broadcast_to(pair_values[:, None], (pair_count, subs, local_len, HD)).reshape(
                seq_count, local_len, HD
            ),
            pair_queries,
        ],
        axis=1,
    )
    received = lax.all_to_all(send, "seq", 0, 0, tiled=True)
    key_piece = received[:, :local_len].reshape(seq_count * local_len, HD)
    value_piece = received[:, local_len : 2 * local_len].reshape(seq_count * local_len, HD)
    query_piece = received[:, 2 * local_len :].reshape(seq_count * sub_rows, HD)
    my_prompt = seq_pos // subs // heads_local
    width_keys = key_piece.shape[0]
    where_global = jnp.arange(width_keys, dtype=jnp.int32)
    shard_index = where_global // local_len
    within = where_global % local_len
    text_index = shard_index * text_rows + within
    key_live = (within >= text_rows) | (text_index < lengths[my_prompt])
    scores = (
        jnp.dot(query_piece, key_piece.T, preferred_element_type=jnp.float32) * scale_factor
    )
    scores = jnp.where(key_live[None, :], scores, -1e30)
    top_score = jnp.max(scores, axis=-1, keepdims=True)
    weights = jnp.exp(scores - top_score)
    denominator = jnp.sum(weights, axis=-1, keepdims=True)
    numerator = jnp.dot(
        weights.astype(jnp.bfloat16), value_piece, preferred_element_type=jnp.float32
    )
    mixed = (numerator / denominator).astype(jnp.bfloat16).reshape(seq_count, sub_rows, HD)
    returned = lax.all_to_all(mixed, "seq", 0, 0, tiled=True)
    attended = returned.reshape(prompts, heads_local, local_len, HD)
    attended = attended.transpose(0, 2, 1, 3).reshape(row_count, heads_local * HD)
    activated = jax.nn.gelu(mlp_units, approximate=True).astype(jnp.bfloat16)
    block_terms = jnp.einsum(
        "bjk,rk->brj",
        attn_weight_t.reshape(wblk_count, dim_local, -1),
        attended,
        preferred_element_type=jnp.float32,
    ) + jnp.einsum(
        "bjk,rk->brj",
        out_weight_t.reshape(wblk_count, dim_local, -1),
        activated,
        preferred_element_type=jnp.float32,
    )
    branch = lax.psum_scatter(
        block_terms.astype(jnp.bfloat16), "wblk", scatter_dimension=0, tiled=True
    )
    branch = branch.reshape(prompts, local_len, dim_local).astype(jnp.float32)
    layer_out = hidden + modulation[2] * branch
    text_out = layer_out[:, :text_rows].astype(jnp.bfloat16)[None]
    image_out = layer_out[:, text_rows:]
    own_prompts = prompts // 2
    rounded_out = image_out.astype(jnp.bfloat16)
    kept = lax.dynamic_slice_in_dim(rounded_out, cfg_pos * own_prompts, own_prompts, 0)
    given = lax.dynamic_slice_in_dim(rounded_out, (1 - cfg_pos) * own_prompts, own_prompts, 0)
    taken = lax.ppermute(given, "cfg", [(0, 1), (1, 0)]).astype(jnp.float32)
    kept = kept.astype(jnp.float32)
    conditional = jnp.where(cfg_pos == 0, kept, taken)
    unconditional = jnp.where(cfg_pos == 0, taken, kept)
    velocity = unconditional + guidance * (conditional - unconditional)
    latent = lax.dynamic_slice_in_dim(image_tokens, cfg_pos * own_prompts, own_prompts, 0).astype(
        jnp.float32
    )
    new_image = latent + step_size * velocity
    return (text_out, velocity, new_image)


def solution(mesh):
    in_specs = (
        P("cfg", None, "seq", "wblk"),
        P(None, "seq", "wblk"),
        P("cfg", "seq"),
        P("seq", None, "wblk"),
        P("seq", None, "wblk", None),
        P("seq", "wblk"),
        P(),
        P(),
        P("wblk", "seq"),
        P("wblk", "seq"),
        P(),
        P(),
    )
    out_specs = (P("cfg", None, "seq", "wblk"), P("cfg", "seq", "wblk"), P("cfg", "seq", "wblk"))
    return jax.shard_map(shards, mesh=mesh, in_specs=in_specs, out_specs=out_specs, check_vma=False)
```
